128 devices in a mesh: req: 16 (over y, x), cache: 8 (over z, core).
Axes of the slice: x: 4, y: 4, z: 4, core: 2. Of those that a mesh axis runs over, the one named last changes fastest.
Arguments:
- cand_x: bfloat16 [32768, 1024], P(('req', 'cache')), may hold values from -6 to 6
- cand_req: int32 [32768, 1], P(('req', 'cache')), may hold values from 0 to 127; in each aligned block of 256 rows (0 to 255, 256 to 511, ...) at most 4 rows name the same one
- hist_len: int32 [128], P(('req', 'cache')), may hold values from 1 to 2048, 131072 in all
- block_place: int32 [128, 128], P(('req', 'cache')), may hold values from 0 to 127, each once within a row
- kv_store: bfloat16 [128, 128, 1, 16, 2048], P(('req', 'cache')), may hold values from -6 to 6
- store_bucket: int32 [128, 128, 1, 16], P(('req', 'cache')), may hold values from 1 to 127
- w_proj: bfloat16 [1024, 2048], replicated, may hold values from -0.1875 to 0.1875
- w_out: bfloat16 [1024, 1024], replicated, may hold values from -0.1875 to 0.1875
- time_bias: float32 [8, 128], replicated, may hold values from -4 to 4
Outputs:
- scored: bfloat16 [32768, 1024], P(('req', 'cache'))
The draws below stay inside these ranges and needn't reach their ends.
Inputs may be any that keep to these rules, and one draw needn't show every extreme that they name: `cand_req`: among the 256 candidate rows of one device at most 4 belong to one request, and some request of some device has exactly 4. `hist_len`: the lengths sum to 131072. `block_place`: each row is a permutation of 0 to 127.
All inputs are finite; a program needn't handle non-finite values. No bound on the sum of `hist_len` on one device may be relied on, other than what follows from the above.
Results may differ from the reference program's by a relative error of at most 0.0055.
Values may be sent and summed in bfloat16 or wider, within the bound.
No kernel may reach another device: no remote copies, remote signals or barrier semaphores. Data moves between devices by JAX's collectives and lax.ppermute only.
A program may use at most 128 MiB of HBM per device.

```python
import math
import jax
import jax.numpy as jnp
import numpy as np
from jax import lax

D = 1024
HEADS = 8
HEAD_DIM = 128
NBUCKET = 128
BLOCK_EV = 16
MAXH = 2048
CAND_DEV = 256
NREQ = 128
NCAND = 32768
CAP = 4
SLOTS = 512
MAXB = 128
CAP_B = 1


def touch_ends(entries, rng, smallest, top_value):
    shape = entries.shape
    spot = [jax.random.randint(jax.random.fold_in(rng, axis), (), 0, shape[axis]) for axis in range(len(shape))]
    entries = entries.at[tuple(spot)].set(smallest)
    longest = shape.index(max(shape))
    spot[longest] = (spot[longest] + 1) % shape[longest]
    return entries.at[tuple(spot)].set(top_value)


def block_scale(stream_key, shape, pieces, low, high):
    factor_of, own = 1.0, jax.random.fold_in(stream_key, 6)
    for dim, blocks in pieces:
        heights = jnp.exp(jax.random.uniform(jax.random.fold_in(own, dim), (blocks,), jnp.float32, low / len(pieces), high / len(pieces)))
        factor_of = factor_of * jnp.repeat(heights, shape[dim] // blocks).reshape([-1 if axis == dim else 1 for axis in range(len(shape))])
    return factor_of


def profile(count, total, reach, skew):
    weights = [(1 << 20) // math.isqrt(standing ** skew) + 1 for standing in range(2, count + 1)]
    rest, counts = total - reach - (count - 1), [1] * (count - 1)
    while rest > 0:
        free = [i for i in range(count - 1) if counts[i] < reach]
        mass, left = sum([weights[i] for i in free]), rest
        for i in free:
            more = min(reach - counts[i], max(1, left * weights[i] // mass), rest)
            counts[i] = counts[i] + more
            rest = rest - more
    return np.array([reach] + counts)


def ragged(own_key, number_of, total, reach, lean):
    if number_of == 2:
        one = jax.random.randint(own_key, (), max(1, total - reach), min(reach, total - 1) + 1)
        return jnp.stack([one, total - one])
    lengths = jnp.asarray(profile(number_of, total, reach, lean), jnp.int32)
    pairs = (number_of - 1) // 2
    donor, taker = lengths[1:1 + 2 * pairs:2], lengths[2:2 + 2 * pairs:2]
    margin = jnp.minimum(donor - 1, reach - taker)
    moved = jax.random.randint(jax.random.fold_in(own_key, 1), (pairs,), 0, 1 << 20) % (margin + 1)
    lengths = lengths.at[1:1 + 2 * pairs:2].set(donor - moved).at[2:2 + 2 * pairs:2].set(taker + moved)
    return lengths[jax.random.permutation(jax.random.fold_in(own_key, 2), number_of)]


def routed_block(key, own, number, rows, count, top, most, lean):
    order = jax.random.permutation(key, count)
    packed, ordinary = portions_of(count, rows * top, most, lean, True), portions_of(count, rows * top, most, lean, False)
    places = jnp.arange(count)

    def named(lengths, turn):
        used = int((lengths > 0).sum())
        fixed = max(1, used // 4)
        moved = fixed + (places - fixed + turn * (used - fixed)) % max(1, count - fixed)
        return jnp.zeros((count,), jnp.int32).at[order[jnp.where(places < fixed, places, moved)]].set(jnp.asarray(lengths, jnp.int32))

    lengths = jnp.where(number % 4 == 0, named(packed, number // 4), named(ordinary, number - number // 4 - 1))
    mixed = jax.random.permutation(jax.random.fold_in(own, 3), count)
    giver, sink = mixed[0:count // 2 * 2:2], mixed[1:count // 2 * 2:2]
    room = jnp.minimum(lengths[giver] - 1, most - lengths[sink]) // 2
    room = jnp.where((giver == order[0]) | (sink == order[0]) | (lengths[sink] == 0), 0, jnp.maximum(room, 0))
    moved = jax.random.randint(jax.random.fold_in(own, 4), (count // 2,), 0, 1 << 20) % (room + 1)
    lengths = lengths.at[giver].add(-moved).at[sink].add(moved)
    labels = jnp.searchsorted(jnp.cumsum(lengths), jnp.arange(rows * top), side="right").astype(jnp.int32)
    table = labels.reshape(top, rows).T
    table = table[jax.random.permutation(jax.random.fold_in(own, 1), rows)]
    turn = jax.random.randint(jax.random.fold_in(own, 2), (rows, 1), 0, top)
    return jnp.take_along_axis(table, (jnp.arange(top)[None, :] + turn) % top, axis=1)


def portions_of(count, total, bound, skew, full):
    portions = [(1 << 20) // math.isqrt(standing ** skew) + 1 for standing in range(1, count + 1)]
    largest = bound if full else min(bound, max(-(-total // count), total * portions[0] // sum(portions)))
    least = 1 if total - largest >= count - 1 else 0
    holding, rest = [largest] + [least] * (count - 1), total - largest - least * (count - 1)
    while rest > 0:
        movable = [i for i in range(1, count) if holding[i] < largest] or [i for i in range(1, count) if holding[i] < bound]
        pool, left = sum([portions[i] for i in movable]), rest
        for i in movable:
            addition = min(bound - holding[i], max(1, left * portions[i] // pool), rest)
            holding[i] = holding[i] + addition
            rest = rest - addition
    return np.array(holding)


def gaussian(key, extent, scale, bound, cuts=(), kind=jnp.bfloat16):
    result = jax.random.normal(key, extent, jnp.float32) * scale
    if len(cuts) > 0:
        result = block_scale(key, extent, cuts, -0.22, 0.18) * result
    return jnp.clip(result, min=-bound, max=bound).astype(kind)


def setup_inputs(seed: int = 0) -> dict:
    key_list = jax.random.split(jax.random.key(seed), 10)
    cand_x = gaussian(key_list[0], (NCAND, D), 1.0, 6.0, ((0, 128),))
    cand_req_keys = jax.random.split(jax.random.fold_in(key_list[1], 1), NCAND // CAND_DEV)
    cand_req_turns = jax.random.permutation(jax.random.fold_in(key_list[1], 3), NCAND // CAND_DEV)
    cand_req = jax.vmap(lambda own, number: routed_block(jax.random.fold_in(key_list[1], 2), own, number, CAND_DEV, NREQ, 1, CAP, 1))(cand_req_keys, cand_req_turns).reshape((NCAND, 1))
    hist_len = ragged(key_list[2], NREQ, NREQ * MAXH // 2, MAXH, 2).astype(jnp.int32)
    block_place = jax.vmap(lambda own: jax.random.permutation(own, MAXB))(jax.random.split(key_list[3], NREQ)).reshape((NREQ, MAXB)).astype(jnp.int32)
    kv_store = gaussian(key_list[4], (NREQ, NREQ, CAP_B, BLOCK_EV, 2 * D), 1.0, 6.0, ((0, 128),))
    store_bucket = touch_ends(jax.random.randint(key_list[5], (NREQ, NREQ, CAP_B, BLOCK_EV), 1, NBUCKET), jax.random.fold_in(key_list[5], 1), 1, NBUCKET - 1).astype(jnp.int32)
    w_proj = gaussian(key_list[6], (D, 2 * D), D ** -0.5, 0.1875)
    w_out = gaussian(key_list[7], (D, D), D ** -0.5, 0.1875)
    time_bias = gaussian(key_list[8], (HEADS, NBUCKET), 1.0, 4.0, (), jnp.float32)
    return {"cand_x": cand_x, "cand_req": cand_req, "hist_len": hist_len, "block_place": block_place, "kv_store": kv_store, "store_bucket": store_bucket, "w_proj": w_proj, "w_out": w_out, "time_bias": time_bias}


def layer_norm(values):
    average = lax.optimization_barrier(jnp.mean(values, axis=-1, keepdims=True))
    centred = values - average
    spread = lax.optimization_barrier(jnp.mean(centred * centred, axis=-1, keepdims=True))
    return centred * lax.rsqrt(spread + 1e-05)

def reference(cand_x, cand_req, hist_len, block_place, kv_store, store_bucket, w_proj, w_out, time_bias):
    normed = layer_norm(cand_x.astype(jnp.float32)).astype(jnp.bfloat16)
    projected = jax.nn.silu(jnp.dot(normed, w_proj, preferred_element_type=jnp.float32)).astype(jnp.bfloat16)
    target = cand_req[:, 0].astype(jnp.int32)
    onehot = (target[:, None] == jnp.arange(NREQ, dtype=jnp.int32)[None, :]).astype(jnp.int32)
    onehot_blocks = onehot.reshape(NREQ, CAND_DEV, NREQ)
    earlier = jnp.cumsum(onehot_blocks, axis=1) - onehot_blocks
    slot_rank = lax.optimization_barrier(jnp.sum(earlier * onehot_blocks, axis=2)).reshape(NCAND).astype(jnp.int32)
    source = jnp.arange(NCAND, dtype=jnp.int32) // CAND_DEV
    flat_slot = (target * SLOTS + source * CAP + slot_rank).astype(jnp.int32)
    row_of_slot = jnp.full((NREQ * SLOTS,), NCAND, jnp.int32).at[flat_slot].set(jnp.arange(NCAND, dtype=jnp.int32))
    padded = jnp.concatenate([projected, jnp.zeros((1, 2 * D), jnp.bfloat16)], axis=0)
    score_scale = 1.0 / math.sqrt(HEAD_DIM)
    position = (jnp.arange(MAXB, dtype=jnp.int32)[:, None] * BLOCK_EV + jnp.arange(BLOCK_EV, dtype=jnp.int32)[None, :]).reshape(MAXH)

    def one_request(request):
        picked = lax.dynamic_slice_in_dim(row_of_slot, (request * SLOTS).astype(jnp.int32), SLOTS)
        slot_proj = jnp.take(padded, picked, axis=0)
        gate_u = slot_proj[:, :D].astype(jnp.float32)
        query = slot_proj[:, D:].astype(jnp.float32).reshape(SLOTS, HEADS, HEAD_DIM)
        places = block_place[request]
        owner = places // CAP_B
        inner = places % CAP_B
        blocks = kv_store[owner, request, inner]
        buckets = store_bucket[owner, request, inner].reshape(MAXH)
        live = (position < hist_len[request]).astype(jnp.float32)
        keys = blocks[:, :, :D].reshape(MAXH, HEADS, HEAD_DIM).astype(jnp.float32)
        values = blocks[:, :, D:].reshape(MAXH, HEADS, HEAD_DIM).astype(jnp.float32)
        bias = time_bias[:, buckets]
        scores = jnp.einsum('shd,ehd->hse', query, keys, precision=lax.Precision.HIGHEST) * score_scale + bias[:, None, :]
        weight = (jax.nn.silu(scores) * live[None, None, :]).astype(jnp.bfloat16)
        attended = jnp.einsum('hse,ehd->shd', weight.astype(jnp.float32), values, precision=lax.Precision.HIGHEST).reshape(SLOTS, D)
        hidden = (layer_norm(attended) * gate_u).astype(jnp.bfloat16)
        return jnp.dot(hidden, w_out, preferred_element_type=jnp.float32).astype(jnp.bfloat16)
    results = lax.map(one_request, jnp.arange(NREQ, dtype=jnp.int32))
    update = results.reshape(NREQ * SLOTS, D)[flat_slot]
    return (cand_x.astype(jnp.float32) + update.astype(jnp.float32)).astype(jnp.bfloat16)
```

```python
import functools
import math

import jax
import jax.numpy as jnp
from jax import lax
from jax.experimental import pallas as pl
from jax.experimental.pallas import tpu as pltpu
from jax.sharding import PartitionSpec as P


def layer_norm(values):
    average = jnp.mean(values, axis=-1, keepdims=True)
    centred = values - average
    spread = jnp.mean(centred * centred, axis=-1, keepdims=True)
    return centred * lax.rsqrt(spread + 1e-05)


def prepare(inputs, w_proj):
    normed = layer_norm(inputs.astype(jnp.float32)).astype(jnp.bfloat16)
    return jax.nn.silu(jnp.dot(normed, w_proj, preferred_element_type=jnp.float32)).astype(
        jnp.bfloat16
    )


def attend_kernel(q_ref, k_ref, v_ref, bias_ref, live_ref, o_ref, *, scale, chunk):
    head = pl.program_id(0)
    query = q_ref[...]
    bias_row = bias_ref[pl.ds(head, 1), :]
    live_row = live_ref[...]
    event_count = k_ref.shape[0]
    acc = jnp.zeros(o_ref.shape, jnp.float32)
    for c in range(event_count // chunk):
        lo = c * chunk
        key = k_ref[pl.ds(lo, chunk), :]
        value = v_ref[pl.ds(lo, chunk), :]
        scores = lax.dot_general(
            query, key, (((1,), (1,)), ((), ())), preferred_element_type=jnp.float32
        )
        scores = scores * scale + bias_row[:, lo : lo + chunk]
        silu = scores / (1.0 + jnp.exp(-scores))
        weight = jnp.where(live_row[:, lo : lo + chunk] > 0.0, silu, 0.0).astype(jnp.bfloat16)
        acc = acc + jnp.dot(weight, value, preferred_element_type=jnp.float32)
    o_ref[...] = acc


def attend(projected, events, bias, live, head_count, head_dim, scale):
    slot_count = projected.shape[0]
    event_count = events.shape[0]
    features = head_count * head_dim
    slot_tile = 256 if slot_count % 256 == 0 else slot_count
    chunk = 512 if event_count % 512 == 0 else event_count
    kernel = functools.partial(attend_kernel, scale=scale, chunk=chunk)
    return pl.pallas_call(
        kernel,
        grid=(head_count, slot_count // slot_tile),
        in_specs=[
            pl.BlockSpec((slot_tile, head_dim), lambda h, i: (i, head_count + h)),
            pl.BlockSpec((event_count, head_dim), lambda h, i: (0, h)),
            pl.BlockSpec((event_count, head_dim), lambda h, i: (0, head_count + h)),
            pl.BlockSpec(bias.shape, lambda h, i: (0, 0)),
            pl.BlockSpec(live.shape, lambda h, i: (0, 0)),
        ],
        out_specs=pl.BlockSpec((slot_tile, head_dim), lambda h, i: (i, h)),
        out_shape=jax.ShapeDtypeStruct((slot_count, features), jnp.float32),
    )(projected, events, events, bias, live)


def shards(
    cand_x, cand_req, hist_len, block_place, kv_store, store_bucket, w_proj, w_out, time_bias
):
    axes = ("req", "cache")
    devices = lax.axis_size(axes)
    row_count = cand_x.shape[0]
    features = cand_x.shape[1]
    head_count = time_bias.shape[0]
    head_dim = features // head_count
    bucket_count = time_bias.shape[1]
    per_owner = kv_store.shape[2]
    block_ev = kv_store.shape[3]
    capacity = max(2, 2 * row_count // devices)
    arrived = lax.all_to_all(kv_store, axes, split_axis=1, concat_axis=0, tiled=True)
    event_count = devices * per_owner * block_ev
    events = arrived.reshape(event_count, 2 * features)

    target = cand_req[:, 0]
    onehot = (target[:, None] == jnp.arange(devices, dtype=jnp.int32)[None, :]).astype(jnp.int32)
    earlier = jnp.cumsum(onehot, axis=0) - onehot
    slot_rank = jnp.sum(earlier * onehot, axis=1)
    flat_slot = target * capacity + slot_rank
    empty = jnp.zeros((devices * capacity, features), cand_x.dtype)
    slotted = empty.at[flat_slot].set(cand_x).reshape(devices, capacity * features)
    bucket_send = store_bucket.reshape(devices, per_owner * block_ev).astype(cand_x.dtype)
    received = lax.all_to_all(
        jnp.concatenate([slotted, bucket_send], axis=1), axes, split_axis=0, concat_axis=0, tiled=True
    )
    senders = received.shape[0]
    flat_rows = received[:, : capacity * features].reshape(senders * capacity, features)
    buckets = received[:, capacity * features :].astype(jnp.int32).reshape(event_count)

    places = block_place[0]
    block_count = places.shape[0]
    block_ids = jnp.arange(block_count, dtype=jnp.int32)
    match = (places[:, None] == block_ids[None, :]).astype(jnp.int32)
    block_of_place = jnp.sum(match * block_ids[:, None], axis=0)
    position = (
        block_of_place[:, None] * block_ev + jnp.arange(block_ev, dtype=jnp.int32)[None, :]
    ).reshape(1, event_count)
    live = (position < hist_len[0]).astype(jnp.float32)
    bucket_table = (buckets[None, :] == jnp.arange(bucket_count, dtype=jnp.int32)[:, None]).astype(
        jnp.float32
    )
    bias = jnp.dot(time_bias, bucket_table, precision=lax.Precision.HIGHEST)
    score_scale = 1.0 / math.sqrt(head_dim)

    projected = prepare(flat_rows, w_proj)
    slot_count = projected.shape[0]
    gate_u = projected[:, :features]
    attended = attend(projected, events, bias, live, head_count, head_dim, score_scale)
    hidden = (layer_norm(attended) * gate_u.astype(jnp.float32)).astype(jnp.bfloat16)
    update = (
        jnp.dot(hidden, w_out, preferred_element_type=jnp.float32)
        .astype(jnp.bfloat16)
        .reshape(senders, capacity, features)
    )
    returned = lax.all_to_all(update, axes, split_axis=0, concat_axis=0, tiled=True)
    update = returned.reshape(devices * capacity, features)[flat_slot]
    return (cand_x.astype(jnp.float32) + update.astype(jnp.float32)).astype(jnp.bfloat16)


def solution(mesh):
    placed = (
        P(("req", "cache"), None),
        P(("req", "cache"), None),
        P(("req", "cache")),
        P(("req", "cache"), None),
        P(("req", "cache"), None, None, None, None),
        P(("req", "cache"), None, None, None),
        P(),
        P(),
        P(),
    )
    return jax.shard_map(
        shards, mesh=mesh, in_specs=placed, out_specs=P(("req", "cache"), None), check_vma=False
    )
```

```python
import functools
import math

import jax
import jax.numpy as jnp
from jax import lax
from jax.experimental import pallas as pl
from jax.experimental.pallas import tpu as pltpu
from jax.sharding import PartitionSpec as P


def layer_norm(values):
    average = jnp.mean(values, axis=-1, keepdims=True)
    centred = values - average
    spread = jnp.mean(centred * centred, axis=-1, keepdims=True)
    return centred * lax.rsqrt(spread + 1e-05)


def prepare(inputs, w_proj):
    normed = layer_norm(inputs.astype(jnp.float32)).astype(jnp.bfloat16)
    return jax.nn.silu(jnp.dot(normed, w_proj, preferred_element_type=jnp.float32)).astype(
        jnp.bfloat16
    )


def attend_kernel(q_ref, k_ref, v_ref, bias_ref, live_ref, o_ref, *, half_scale, chunk):
    head = pl.program_id(0)
    query = q_ref[...]
    bias_row = bias_ref[pl.ds(head, 1), :]
    event_count = k_ref.shape[0]
    acc = jnp.zeros(o_ref.shape, jnp.float32)
    for c in range(event_count // chunk):
        lo = c * chunk
        key = k_ref[pl.ds(lo, chunk), :]
        value = v_ref[pl.ds(lo, chunk), :]
        value = jnp.where(live_ref[pl.ds(lo, chunk), :] > 0.0, value, jnp.zeros_like(value))
        scores = lax.dot_general(
            query, key, (((1,), (1,)), ((), ())), preferred_element_type=jnp.float32
        )
        half = scores * half_scale + bias_row[:, lo : lo + chunk]
        weight = (half + half * jnp.tanh(half)).astype(jnp.bfloat16)
        acc = acc + jnp.dot(weight, value, preferred_element_type=jnp.float32)
    o_ref[...] = acc


def attend(projected, events, half_bias, live, head_count, head_dim, half_scale):
    slot_count = projected.shape[0]
    event_count = events.shape[0]
    features = head_count * head_dim
    chunk = 512 if event_count % 512 == 0 else event_count
    kernel = functools.partial(attend_kernel, half_scale=half_scale, chunk=chunk)
    return pl.pallas_call(
        kernel,
        grid=(head_count,),
        in_specs=[
            pl.BlockSpec((slot_count, head_dim), lambda h: (0, head_count + h)),
            pl.BlockSpec((event_count, head_dim), lambda h: (0, h)),
            pl.BlockSpec((event_count, head_dim), lambda h: (0, head_count + h)),
            pl.BlockSpec(half_bias.shape, lambda h: (0, 0)),
            pl.BlockSpec(live.shape, lambda h: (0, 0)),
        ],
        out_specs=pl.BlockSpec((slot_count, head_dim), lambda h: (0, h)),
        out_shape=jax.ShapeDtypeStruct((slot_count, features), jnp.float32),
    )(projected, events, events, half_bias, live)


def shards(
    cand_x, cand_req, hist_len, block_place, kv_store, store_bucket, w_proj, w_out, time_bias
):
    axes = ("req", "cache")
    devices = lax.axis_size(axes)
    row_count = cand_x.shape[0]
    features = cand_x.shape[1]
    head_count = time_bias.shape[0]
    head_dim = features // head_count
    bucket_count = time_bias.shape[1]
    per_owner = kv_store.shape[2]
    block_ev = kv_store.shape[3]
    capacity = max(2, 2 * row_count // devices)
    event_count = devices * per_owner * block_ev
    kv_send = kv_store.reshape(devices, per_owner * block_ev, 2 * features)

    target = cand_req[:, 0]
    onehot = (target[:, None] == jnp.arange(devices, dtype=jnp.int32)[None, :]).astype(jnp.int32)
    earlier = jnp.cumsum(onehot, axis=0) - onehot
    slot_rank = jnp.sum(earlier * onehot, axis=1)
    flat_slot = target * capacity + slot_rank
    empty = jnp.zeros((devices * capacity, features), cand_x.dtype)
    rows_per = per_owner * block_ev
    slotted = empty.at[flat_slot].set(cand_x).reshape(devices, rows_per, capacity * features // rows_per)
    bucket_send = store_bucket.reshape(devices, rows_per, 1).astype(cand_x.dtype)
    received = lax.all_to_all(
        jnp.concatenate([kv_send, slotted, bucket_send], axis=2),
        axes,
        split_axis=0,
        concat_axis=0,
        tiled=True,
    )
    senders = received.shape[0]
    width = received.shape[2]
    events = received.reshape(event_count, width)
    flat_rows = received[:, :, 2 * features : width - 1].reshape(senders * capacity, features)
    buckets = received[:, :, width - 1].astype(jnp.int32).reshape(event_count)

    places = block_place[0]
    block_count = places.shape[0]
    block_ids = jnp.arange(block_count, dtype=jnp.int32)
    match = (places[:, None] == block_ids[None, :]).astype(jnp.int32)
    block_of_place = jnp.sum(match * block_ids[:, None], axis=0)
    position = (
        block_of_place[:, None] * block_ev + jnp.arange(block_ev, dtype=jnp.int32)[None, :]
    ).reshape(event_count, 1)
    live = (position < hist_len[0]).astype(jnp.float32)
    bucket_table = (buckets[None, :] == jnp.arange(bucket_count, dtype=jnp.int32)[:, None]).astype(
        jnp.float32
    )
    half_bias = 0.5 * jnp.dot(time_bias, bucket_table, precision=lax.Precision.HIGHEST)
    half_scale = 0.5 / math.sqrt(head_dim)

    projected = prepare(flat_rows, w_proj)
    slot_count = projected.shape[0]
    gate_u = projected[:, :features]
    attended = attend(projected, events, half_bias, live, head_count, head_dim, half_scale)
    hidden = (layer_norm(attended) * gate_u.astype(jnp.float32)).astype(jnp.bfloat16)
    update = (
        jnp.dot(hidden, w_out, preferred_element_type=jnp.float32)
        .astype(jnp.bfloat16)
        .reshape(senders, capacity, features)
    )
    returned = lax.all_to_all(update, axes, split_axis=0, concat_axis=0, tiled=True)
    update = returned.reshape(devices * capacity, features)[flat_slot]
    return (cand_x.astype(jnp.float32) + update.astype(jnp.float32)).astype(jnp.bfloat16)


def solution(mesh):
    placed = (
        P(("req", "cache"), None),
        P(("req", "cache"), None),
        P(("req", "cache")),
        P(("req", "cache"), None),
        P(("req", "cache"), None, None, None, None),
        P(("req", "cache"), None, None, None),
        P(),
        P(),
        P(),
    )
    return jax.shard_map(
        shards, mesh=mesh, in_specs=placed, out_specs=P(("req", "cache"), None), check_vma=False
    )
```

```python
import functools
import math

import jax
import jax.numpy as jnp
from jax import lax
from jax.experimental import pallas as pl
from jax.experimental.pallas import tpu as pltpu
from jax.sharding import PartitionSpec as P


def layer_norm(values):
    average = jnp.mean(values, axis=-1, keepdims=True)
    centred = values - average
    spread = jnp.mean(centred * centred, axis=-1, keepdims=True)
    return centred * lax.rsqrt(spread + 1e-05)


def prepare(inputs, w_proj):
    normed = layer_norm(inputs.astype(jnp.float32)).astype(jnp.bfloat16)
    return jax.nn.silu(jnp.dot(normed, w_proj, preferred_element_type=jnp.float32)).astype(
        jnp.bfloat16
    )


def attend_kernel(q_ref, k_ref, v_ref, bias_ref, live_ref, o_ref, *, half_scale, chunk):
    head = pl.program_id(0)
    query = q_ref[...]
    bias_row = bias_ref[pl.ds(head, 1), :]
    event_count = k_ref.shape[0]
    acc = jnp.zeros(o_ref.shape, jnp.float32)
    for c in range(event_count // chunk):
        lo = c * chunk
        key = k_ref[pl.ds(lo, chunk), :]
        value = v_ref[pl.ds(lo, chunk), :]
        value = jnp.where(live_ref[pl.ds(lo, chunk), :] > 0.0, value, jnp.zeros_like(value))
        scores = lax.dot_general(
            query, key, (((1,), (1,)), ((), ())), preferred_element_type=jnp.float32
        )
        half = scores * half_scale + bias_row[:, lo : lo + chunk]
        weight = (half + half * jnp.tanh(half)).astype(jnp.bfloat16)
        acc = acc + jnp.dot(weight, value, preferred_element_type=jnp.float32)
    o_ref[...] = acc


def attend(projected, events, half_bias, live, head_count, head_dim, half_scale):
    slot_count = projected.shape[0]
    event_count = events.shape[0]
    features = head_count * head_dim
    chunk = 512 if event_count % 512 == 0 else event_count
    kernel = functools.partial(attend_kernel, half_scale=half_scale, chunk=chunk)
    return pl.pallas_call(
        kernel,
        grid=(head_count,),
        in_specs=[
            pl.BlockSpec((slot_count, head_dim), lambda h: (0, head_count + h)),
            pl.BlockSpec((event_count, head_dim), lambda h: (0, h)),
            pl.BlockSpec((event_count, head_dim), lambda h: (0, head_count + h)),
            pl.BlockSpec(half_bias.shape, lambda h: (0, 0)),
            pl.BlockSpec(live.shape, lambda h: (0, 0)),
        ],
        out_specs=pl.BlockSpec((slot_count, head_dim), lambda h: (0, h)),
        out_shape=jax.ShapeDtypeStruct((slot_count, features), jnp.float32),
    )(projected, events, events, half_bias, live)


def shards(
    cand_x, cand_req, hist_len, block_place, kv_store, store_bucket, w_proj, w_out, time_bias
):
    axes = ("req", "cache")
    devices = lax.axis_size(axes)
    row_count = cand_x.shape[0]
    features = cand_x.shape[1]
    head_count = time_bias.shape[0]
    head_dim = features // head_count
    bucket_count = time_bias.shape[1]
    per_owner = kv_store.shape[2]
    block_ev = kv_store.shape[3]
    capacity = max(2, 2 * row_count // devices)
    event_count = devices * per_owner * block_ev
    arrived = lax.all_to_all(kv_store, axes, split_axis=1, concat_axis=0, tiled=True)
    events = arrived.reshape(event_count, 2 * features)
    every_bucket = lax.all_gather(store_bucket, axes, axis=0, tiled=True)
    me = lax.axis_index(axes)
    buckets = lax.dynamic_index_in_dim(every_bucket, me, axis=1, keepdims=False).reshape(event_count)

    target = cand_req[:, 0]
    onehot = (target[:, None] == jnp.arange(devices, dtype=jnp.int32)[None, :]).astype(jnp.int32)
    earlier = jnp.cumsum(onehot, axis=0) - onehot
    slot_rank = jnp.sum(earlier * onehot, axis=1)
    flat_slot = target * capacity + slot_rank
    empty = jnp.zeros((devices * capacity, features), cand_x.dtype)
    received = lax.all_to_all(
        empty.at[flat_slot].set(cand_x).reshape(devices, capacity, features),
        axes,
        split_axis=0,
        concat_axis=0,
        tiled=True,
    )
    senders = received.shape[0]
    flat_rows = received.reshape(senders * capacity, features)

    places = block_place[0]
    block_count = places.shape[0]
    block_ids = jnp.arange(block_count, dtype=jnp.int32)
    match = (places[:, None] == block_ids[None, :]).astype(jnp.int32)
    block_of_place = jnp.sum(match * block_ids[:, None], axis=0)
    position = (
        block_of_place[:, None] * block_ev + jnp.arange(block_ev, dtype=jnp.int32)[None, :]
    ).reshape(event_count, 1)
    live = (position < hist_len[0]).astype(jnp.float32)
    bucket_table = (buckets[None, :] == jnp.arange(bucket_count, dtype=jnp.int32)[:, None]).astype(
        jnp.float32
    )
    half_bias = 0.5 * jnp.dot(time_bias, bucket_table, precision=lax.Precision.HIGHEST)
    half_scale = 0.5 / math.sqrt(head_dim)

    projected = prepare(flat_rows, w_proj)
    slot_count = projected.shape[0]
    gate_u = projected[:, :features]
    attended = attend(projected, events, half_bias, live, head_count, head_dim, half_scale)
    hidden = (layer_norm(attended) * gate_u.astype(jnp.float32)).astype(jnp.bfloat16)
    update = (
        jnp.dot(hidden, w_out, preferred_element_type=jnp.float32)
        .astype(jnp.bfloat16)
        .reshape(senders, capacity, features)
    )
    returned = lax.all_to_all(update, axes, split_axis=0, concat_axis=0, tiled=True)
    update = returned.reshape(devices * capacity, features)[flat_slot]
    return (cand_x.astype(jnp.float32) + update.astype(jnp.float32)).astype(jnp.bfloat16)


def solution(mesh):
    placed = (
        P(("req", "cache"), None),
        P(("req", "cache"), None),
        P(("req", "cache")),
        P(("req", "cache"), None),
        P(("req", "cache"), None, None, None, None),
        P(("req", "cache"), None, None, None),
        P(),
        P(),
        P(),
    )
    return jax.shard_map(
        shards, mesh=mesh, in_specs=placed, out_specs=P(("req", "cache"), None), check_vma=False
    )
```

```python
import functools
import math

import jax
import jax.numpy as jnp
from jax import lax
from jax.experimental import pallas as pl
from jax.experimental.pallas import tpu as pltpu
from jax.sharding import PartitionSpec as P


def layer_norm(values):
    average = jnp.mean(values, axis=-1, keepdims=True)
    centred = values - average
    spread = jnp.mean(centred * centred, axis=-1, keepdims=True)
    return centred * lax.rsqrt(spread + 1e-05)


def prepare(inputs, w_proj):
    normed = layer_norm(inputs.astype(jnp.float32)).astype(jnp.bfloat16)
    return jax.nn.silu(jnp.dot(normed, w_proj, preferred_element_type=jnp.float32)).astype(
        jnp.bfloat16
    )


def attend_kernel(q_ref, k_ref, v_ref, bias_ref, live_ref, o_ref, *, half_scale, chunk):
    head = pl.program_id(0)
    query = q_ref[...]
    bias_row = bias_ref[pl.ds(head, 1), :]
    event_count = k_ref.shape[0]
    acc = jnp.zeros(o_ref.shape, jnp.float32)
    for c in range(event_count // chunk):
        lo = c * chunk
        key = k_ref[pl.ds(lo, chunk), :]
        value = v_ref[pl.ds(lo, chunk), :]
        value = jnp.where(live_ref[pl.ds(lo, chunk), :] > 0.0, value, jnp.zeros_like(value))
        scores = lax.dot_general(
            query, key, (((1,), (1,)), ((), ())), preferred_element_type=jnp.float32
        )
        half = scores * half_scale + bias_row[:, lo : lo + chunk]
        weight = (half + half * jnp.tanh(half)).astype(jnp.bfloat16)
        acc = acc + jnp.dot(weight, value, preferred_element_type=jnp.float32)
    o_ref[...] = acc


def attend(projected, events, half_bias, live, head_count, head_dim, half_scale):
    slot_count = projected.shape[0]
    event_count = events.shape[0]
    features = head_count * head_dim
    chunk = 512 if event_count % 512 == 0 else event_count
    kernel = functools.partial(attend_kernel, half_scale=half_scale, chunk=chunk)
    return pl.pallas_call(
        kernel,
        grid=(head_count,),
        in_specs=[
            pl.BlockSpec((slot_count, head_dim), lambda h: (0, head_count + h)),
            pl.BlockSpec((event_count, head_dim), lambda h: (0, h)),
            pl.BlockSpec((event_count, head_dim), lambda h: (0, head_count + h)),
            pl.BlockSpec(half_bias.shape, lambda h: (0, 0)),
            pl.BlockSpec(live.shape, lambda h: (0, 0)),
        ],
        out_specs=pl.BlockSpec((slot_count, head_dim), lambda h: (0, h)),
        out_shape=jax.ShapeDtypeStruct((slot_count, features), jnp.float32),
    )(projected, events, events, half_bias, live)


def exchange(values):
    outer = lax.axis_size("req")
    inner = lax.axis_size("cache")
    rest = values.shape[1:]
    values = values.reshape((outer, inner) + rest)
    values = lax.all_to_all(values, "cache", split_axis=1, concat_axis=1, tiled=True)
    values = lax.all_to_all(values, "req", split_axis=0, concat_axis=0, tiled=True)
    return values.reshape((outer * inner,) + rest)


def shards(
    cand_x, cand_req, hist_len, block_place, kv_store, store_bucket, w_proj, w_out, time_bias
):
    axes = ("req", "cache")
    devices = lax.axis_size(axes)
    row_count = cand_x.shape[0]
    features = cand_x.shape[1]
    head_count = time_bias.shape[0]
    head_dim = features // head_count
    bucket_count = time_bias.shape[1]
    per_owner = kv_store.shape[2]
    block_ev = kv_store.shape[3]
    capacity = max(2, 2 * row_count // devices)
    event_count = devices * per_owner * block_ev
    arrived = lax.all_to_all(kv_store, axes, split_axis=1, concat_axis=0, tiled=True)
    events = arrived.reshape(event_count, 2 * features)

    target = cand_req[:, 0]
    onehot = (target[:, None] == jnp.arange(devices, dtype=jnp.int32)[None, :]).astype(jnp.int32)
    earlier = jnp.cumsum(onehot, axis=0) - onehot
    slot_rank = jnp.sum(earlier * onehot, axis=1)
    flat_slot = target * capacity + slot_rank
    empty = jnp.zeros((devices * capacity, features), cand_x.dtype)
    slotted = empty.at[flat_slot].set(cand_x).reshape(devices, capacity, features)
    rows_per = per_owner * block_ev
    bucket_lanes = rows_per // capacity
    bucket_send = store_bucket.reshape(devices, capacity, bucket_lanes).astype(cand_x.dtype)
    bucket_send = jnp.pad(bucket_send, ((0, 0), (0, 0), (0, 128 - bucket_lanes)))
    received = exchange(jnp.concatenate([slotted, bucket_send], axis=2))
    senders = received.shape[0]
    flat_rows = received[:, :, :features].reshape(senders * capacity, features)
    buckets = received[:, :, features : features + bucket_lanes].astype(jnp.int32).reshape(event_count)

    places = block_place[0]
    block_count = places.shape[0]
    block_ids = jnp.arange(block_count, dtype=jnp.int32)
    match = (places[:, None] == block_ids[None, :]).astype(jnp.int32)
    block_of_place = jnp.sum(match * block_ids[:, None], axis=0)
    position = (
        block_of_place[:, None] * block_ev + jnp.arange(block_ev, dtype=jnp.int32)[None, :]
    ).reshape(event_count, 1)
    live = (position < hist_len[0]).astype(jnp.float32)
    bucket_table = (buckets[None, :] == jnp.arange(bucket_count, dtype=jnp.int32)[:, None]).astype(
        jnp.float32
    )
    half_bias = 0.5 * jnp.dot(time_bias, bucket_table, precision=lax.Precision.HIGHEST)
    half_scale = 0.5 / math.sqrt(head_dim)

    projected = prepare(flat_rows, w_proj)
    slot_count = projected.shape[0]
    gate_u = projected[:, :features]
    attended = attend(projected, events, half_bias, live, head_count, head_dim, half_scale)
    hidden = (layer_norm(attended) * gate_u.astype(jnp.float32)).astype(jnp.bfloat16)
    update = (
        jnp.dot(hidden, w_out, preferred_element_type=jnp.float32)
        .astype(jnp.bfloat16)
        .reshape(senders, capacity, features)
    )
    returned = exchange(update)
    update = returned.reshape(devices * capacity, features)[flat_slot]
    return (cand_x.astype(jnp.float32) + update.astype(jnp.float32)).astype(jnp.bfloat16)


def solution(mesh):
    placed = (
        P(("req", "cache"), None),
        P(("req", "cache"), None),
        P(("req", "cache")),
        P(("req", "cache"), None),
        P(("req", "cache"), None, None, None, None),
        P(("req", "cache"), None, None, None),
        P(),
        P(),
        P(),
    )
    return jax.shard_map(
        shards, mesh=mesh, in_specs=placed, out_specs=P(("req", "cache"), None), check_vma=False
    )
```

```python
import functools
import math

import jax
import jax.numpy as jnp
from jax import lax
from jax.experimental import pallas as pl
from jax.experimental.pallas import tpu as pltpu
from jax.sharding import PartitionSpec as P


def layer_norm(values):
    average = jnp.mean(values, axis=-1, keepdims=True)
    centred = values - average
    spread = jnp.mean(centred * centred, axis=-1, keepdims=True)
    return centred * lax.rsqrt(spread + 1e-05)


def prepare(inputs, w_proj):
    normed = layer_norm(inputs.astype(jnp.float32)).astype(jnp.bfloat16)
    return jax.nn.silu(jnp.dot(normed, w_proj, preferred_element_type=jnp.float32)).astype(
        jnp.bfloat16
    )


def attend_kernel(q_ref, k_ref, v_ref, bias_ref, live_ref, o_ref, *, half_scale, chunk):
    head = pl.program_id(0)
    query = q_ref[...]
    bias_row = bias_ref[pl.ds(head, 1), :]
    event_count = k_ref.shape[0]
    acc = jnp.zeros(o_ref.shape, jnp.float32)
    for c in range(event_count // chunk):
        lo = c * chunk
        key = k_ref[pl.ds(lo, chunk), :]
        value = v_ref[pl.ds(lo, chunk), :]
        value = jnp.where(live_ref[pl.ds(lo, chunk), :] > 0.0, value, jnp.zeros_like(value))
        scores = lax.dot_general(
            query, key, (((1,), (1,)), ((), ())), preferred_element_type=jnp.float32
        )
        half = scores * half_scale + bias_row[:, lo : lo + chunk]
        weight = (half + half * jnp.tanh(half)).astype(jnp.bfloat16)
        acc = acc + jnp.dot(weight, value, preferred_element_type=jnp.float32)
    o_ref[...] = acc


def attend(projected, events, half_bias, live, head_count, head_dim, half_scale):
    slot_count = projected.shape[0]
    event_count = events.shape[0]
    features = head_count * head_dim
    chunk = 512 if event_count % 512 == 0 else event_count
    kernel = functools.partial(attend_kernel, half_scale=half_scale, chunk=chunk)
    return pl.pallas_call(
        kernel,
        grid=(head_count,),
        in_specs=[
            pl.BlockSpec((slot_count, head_dim), lambda h: (0, h)),
            pl.BlockSpec((event_count, head_dim), lambda h: (0, h)),
            pl.BlockSpec((event_count, head_dim), lambda h: (0, head_count + h)),
            pl.BlockSpec(half_bias.shape, lambda h: (0, 0)),
            pl.BlockSpec(live.shape, lambda h: (0, 0)),
        ],
        out_specs=pl.BlockSpec((slot_count, head_dim), lambda h: (0, h)),
        out_shape=jax.ShapeDtypeStruct((slot_count, features), jnp.float32),
    )(projected, events, events, half_bias, live)


def shards(
    cand_x, cand_req, hist_len, block_place, kv_store, store_bucket, w_proj, w_out, time_bias
):
    axes = ("req", "cache")
    devices = lax.axis_size(axes)
    row_count = cand_x.shape[0]
    features = cand_x.shape[1]
    head_count = time_bias.shape[0]
    head_dim = features // head_count
    bucket_count = time_bias.shape[1]
    per_owner = kv_store.shape[2]
    block_ev = kv_store.shape[3]
    capacity = max(2, 2 * row_count // devices)
    rows_per = per_owner * block_ev
    event_count = devices * rows_per

    projected = prepare(cand_x, w_proj)
    gate_u = projected[:, :features]
    query = projected[:, features:]

    target = cand_req[:, 0]
    onehot = (target[:, None] == jnp.arange(devices, dtype=jnp.int32)[None, :]).astype(jnp.int32)
    earlier = jnp.cumsum(onehot, axis=0) - onehot
    slot_rank = jnp.sum(earlier * onehot, axis=1)
    flat_slot = target * capacity + slot_rank
    empty = jnp.zeros((devices * capacity, features), query.dtype)
    query_width = capacity * features // rows_per
    slotted = empty.at[flat_slot].set(query).reshape(devices, rows_per, query_width)
    kv_send = kv_store.reshape(devices, rows_per, 2 * features)
    bucket_send = store_bucket.reshape(devices, rows_per, 1).astype(cand_x.dtype)
    bucket_send = jnp.pad(bucket_send, ((0, 0), (0, 0), (0, 127)))
    received = lax.all_to_all(
        jnp.concatenate([kv_send, slotted, bucket_send], axis=2),
        axes,
        split_axis=0,
        concat_axis=0,
        tiled=True,
    )
    senders = received.shape[0]
    width = received.shape[2]
    events = received.reshape(event_count, width)
    slot_query = received[:, :, 2 * features : 2 * features + query_width].reshape(
        senders * capacity, features
    )
    buckets = received[:, :, 2 * features + query_width].astype(jnp.int32).reshape(event_count)

    places = block_place[0]
    block_count = places.shape[0]
    block_ids = jnp.arange(block_count, dtype=jnp.int32)
    match = (places[:, None] == block_ids[None, :]).astype(jnp.int32)
    block_of_place = jnp.sum(match * block_ids[:, None], axis=0)
    position = (
        block_of_place[:, None] * block_ev + jnp.arange(block_ev, dtype=jnp.int32)[None, :]
    ).reshape(event_count, 1)
    live = (position < hist_len[0]).astype(jnp.float32)
    bucket_table = (buckets[None, :] == jnp.arange(bucket_count, dtype=jnp.int32)[:, None]).astype(
        jnp.float32
    )
    half_bias = 0.5 * jnp.dot(time_bias, bucket_table, precision=lax.Precision.HIGHEST)
    half_scale = 0.5 / math.sqrt(head_dim)

    attended = attend(slot_query, events, half_bias, live, head_count, head_dim, half_scale)
    normal = layer_norm(attended).astype(jnp.bfloat16).reshape(senders, capacity, features)
    returned = lax.all_to_all(normal, axes, split_axis=0, concat_axis=0, tiled=True)
    normal = returned.reshape(devices * capacity, features)[flat_slot]
    hidden = (normal.astype(jnp.float32) * gate_u.astype(jnp.float32)).astype(jnp.bfloat16)
    update = jnp.dot(hidden, w_out, preferred_element_type=jnp.float32).astype(jnp.bfloat16)
    return (cand_x.astype(jnp.float32) + update.astype(jnp.float32)).astype(jnp.bfloat16)


def solution(mesh):
    placed = (
        P(("req", "cache"), None),
        P(("req", "cache"), None),
        P(("req", "cache")),
        P(("req", "cache"), None),
        P(("req", "cache"), None, None, None, None),
        P(("req", "cache"), None, None, None),
        P(),
        P(),
        P(),
    )
    return jax.shard_map(
        shards, mesh=mesh, in_specs=placed, out_specs=P(("req", "cache"), None), check_vma=False
    )
```

```python
import functools
import math

import jax
import jax.numpy as jnp
from jax import lax
from jax.experimental import pallas as pl
from jax.experimental.pallas import tpu as pltpu
from jax.sharding import PartitionSpec as P


def layer_norm(values):
    average = jnp.mean(values, axis=-1, keepdims=True)
    centred = values - average
    spread = jnp.mean(centred * centred, axis=-1, keepdims=True)
    return centred * lax.rsqrt(spread + 1e-05)


def prepare(inputs, w_proj):
    normed = layer_norm(inputs.astype(jnp.float32)).astype(jnp.bfloat16)
    return jax.nn.silu(jnp.dot(normed, w_proj, preferred_element_type=jnp.float32)).astype(
        jnp.bfloat16
    )


def attend_kernel(q_ref, k_ref, v_ref, bias_ref, live_ref, o_ref, *, half_scale, chunk):
    head = pl.program_id(0)
    query = q_ref[...]
    bias_row = bias_ref[pl.ds(head, 1), :]
    event_count = k_ref.shape[0]
    acc = jnp.zeros(o_ref.shape, jnp.float32)
    for c in range(event_count // chunk):
        lo = c * chunk
        key = k_ref[pl.ds(lo, chunk), :]
        value = v_ref[pl.ds(lo, chunk), :]
        value = jnp.where(live_ref[pl.ds(lo, chunk), :] > 0.0, value, jnp.zeros_like(value))
        scores = lax.dot_general(
            query, key, (((1,), (1,)), ((), ())), preferred_element_type=jnp.float32
        )
        half = scores * half_scale + bias_row[:, lo : lo + chunk]
        weight = (half + half * jnp.tanh(half)).astype(jnp.bfloat16)
        acc = acc + jnp.dot(weight, value, preferred_element_type=jnp.float32)
    o_ref[...] = acc


def attend(projected, events, half_bias, live, head_count, head_dim, half_scale):
    slot_count = projected.shape[0]
    event_count = events.shape[0]
    features = head_count * head_dim
    chunk = 512 if event_count % 512 == 0 else event_count
    kernel = functools.partial(attend_kernel, half_scale=half_scale, chunk=chunk)
    return pl.pallas_call(
        kernel,
        grid=(head_count,),
        in_specs=[
            pl.BlockSpec((slot_count, head_dim), lambda h: (0, head_count + h)),
            pl.BlockSpec((event_count, head_dim), lambda h: (0, h)),
            pl.BlockSpec((event_count, head_dim), lambda h: (0, head_count + h)),
            pl.BlockSpec(half_bias.shape, lambda h: (0, 0)),
            pl.BlockSpec(live.shape, lambda h: (0, 0)),
        ],
        out_specs=pl.BlockSpec((slot_count, head_dim), lambda h: (0, h)),
        out_shape=jax.ShapeDtypeStruct((slot_count, features), jnp.float32),
    )(projected, events, events, half_bias, live)


def shards(
    cand_x, cand_req, hist_len, block_place, kv_store, store_bucket, w_proj, w_out, time_bias
):
    axes = ("req", "cache")
    devices = lax.axis_size(axes)
    row_count = cand_x.shape[0]
    features = cand_x.shape[1]
    head_count = time_bias.shape[0]
    head_dim = features // head_count
    bucket_count = time_bias.shape[1]
    per_owner = kv_store.shape[2]
    block_ev = kv_store.shape[3]
    capacity = max(2, 2 * row_count // devices)
    event_count = devices * per_owner * block_ev
    arrived = lax.all_to_all(kv_store, axes, split_axis=1, concat_axis=0, tiled=True)

    target = cand_req[:, 0]
    onehot = (target[:, None] == jnp.arange(devices, dtype=jnp.int32)[None, :]).astype(jnp.int32)
    earlier = jnp.cumsum(onehot, axis=0) - onehot
    slot_rank = jnp.sum(earlier * onehot, axis=1)
    flat_slot = target * capacity + slot_rank
    empty = jnp.zeros((devices * capacity, features), cand_x.dtype)
    slotted = empty.at[flat_slot].set(cand_x).reshape(devices, capacity, features)
    rows_per = per_owner * block_ev
    bucket_lanes = rows_per // capacity
    bucket_send = store_bucket.reshape(devices, capacity, bucket_lanes).astype(cand_x.dtype)
    bucket_send = jnp.pad(bucket_send, ((0, 0), (0, 0), (0, 128 - bucket_lanes)))
    send = jnp.concatenate([slotted, bucket_send], axis=2)
    arrived, send = lax.optimization_barrier((arrived, send))
    events = arrived.reshape(event_count, 2 * features)
    received = lax.all_to_all(send, axes, split_axis=0, concat_axis=0, tiled=True)
    senders = received.shape[0]
    flat_rows = received[:, :, :features].reshape(senders * capacity, features)
    buckets = received[:, :, features : features + bucket_lanes].astype(jnp.int32).reshape(event_count)

    places = block_place[0]
    block_count = places.shape[0]
    block_ids = jnp.arange(block_count, dtype=jnp.int32)
    match = (places[:, None] == block_ids[None, :]).astype(jnp.int32)
    block_of_place = jnp.sum(match * block_ids[:, None], axis=0)
    position = (
        block_of_place[:, None] * block_ev + jnp.arange(block_ev, dtype=jnp.int32)[None, :]
    ).reshape(event_count, 1)
    live = (position < hist_len[0]).astype(jnp.float32)
    bucket_table = (buckets[None, :] == jnp.arange(bucket_count, dtype=jnp.int32)[:, None]).astype(
        jnp.float32
    )
    half_bias = 0.5 * jnp.dot(time_bias, bucket_table, precision=lax.Precision.HIGHEST)
    half_scale = 0.5 / math.sqrt(head_dim)

    projected = prepare(flat_rows, w_proj)
    slot_count = projected.shape[0]
    gate_u = projected[:, :features]
    attended = attend(projected, events, half_bias, live, head_count, head_dim, half_scale)
    hidden = (layer_norm(attended) * gate_u.astype(jnp.float32)).astype(jnp.bfloat16)
    update = (
        jnp.dot(hidden, w_out, preferred_element_type=jnp.float32)
        .astype(jnp.bfloat16)
        .reshape(senders, capacity, features)
    )
    returned = lax.all_to_all(update, axes, split_axis=0, concat_axis=0, tiled=True)
    update = returned.reshape(devices * capacity, features)[flat_slot]
    return (cand_x.astype(jnp.float32) + update.astype(jnp.float32)).astype(jnp.bfloat16)


def solution(mesh):
    placed = (
        P(("req", "cache"), None),
        P(("req", "cache"), None),
        P(("req", "cache")),
        P(("req", "cache"), None),
        P(("req", "cache"), None, None, None, None),
        P(("req", "cache"), None, None, None),
        P(),
        P(),
        P(),
    )
    return jax.shard_map(
        shards, mesh=mesh, in_specs=placed, out_specs=P(("req", "cache"), None), check_vma=False
    )
```

```python
import functools
import math

import jax
import jax.numpy as jnp
from jax import lax
from jax.experimental import pallas as pl
from jax.experimental.pallas import tpu as pltpu
from jax.sharding import PartitionSpec as P


def layer_norm(values):
    average = jnp.mean(values, axis=-1, keepdims=True)
    centred = values - average
    spread = jnp.mean(centred * centred, axis=-1, keepdims=True)
    return centred * lax.rsqrt(spread + 1e-05)


def prepare(inputs, w_proj):
    normed = layer_norm(inputs.astype(jnp.float32)).astype(jnp.bfloat16)
    return jax.nn.silu(jnp.dot(normed, w_proj, preferred_element_type=jnp.float32)).astype(
        jnp.bfloat16
    )


def attend_kernel(q_ref, k_ref, v_ref, bias_ref, live_ref, o_ref, *, half_scale, chunk):
    head = pl.program_id(0)
    query = q_ref[...]
    bias_row = bias_ref[pl.ds(head, 1), :]
    event_count = k_ref.shape[0]
    acc = jnp.zeros(o_ref.shape, jnp.float32)
    for c in range(event_count // chunk):
        lo = c * chunk
        key = k_ref[pl.ds(lo, chunk), :]
        value = v_ref[pl.ds(lo, chunk), :]
        value = jnp.where(live_ref[pl.ds(lo, chunk), :] > 0.0, value, jnp.zeros_like(value))
        scores = lax.dot_general(
            query, key, (((1,), (1,)), ((), ())), preferred_element_type=jnp.float32
        )
        half = scores * half_scale + bias_row[:, lo : lo + chunk]
        weight = (half + half * jnp.tanh(half)).astype(jnp.bfloat16)
        acc = acc + jnp.dot(weight, value, preferred_element_type=jnp.float32)
    o_ref[...] = acc


def attend(projected, events, half_bias, live, head_count, head_dim, half_scale):
    slot_count = projected.shape[0]
    event_count = events.shape[0]
    features = head_count * head_dim
    chunk = 512 if event_count % 512 == 0 else event_count
    kernel = functools.partial(attend_kernel, half_scale=half_scale, chunk=chunk)
    return pl.pallas_call(
        kernel,
        grid=(head_count,),
        in_specs=[
            pl.BlockSpec((slot_count, head_dim), lambda h: (0, head_count + h)),
            pl.BlockSpec((event_count, head_dim), lambda h: (0, h)),
            pl.BlockSpec((event_count, head_dim), lambda h: (0, head_count + h)),
            pl.BlockSpec(half_bias.shape, lambda h: (0, 0)),
            pl.BlockSpec(live.shape, lambda h: (0, 0)),
        ],
        out_specs=pl.BlockSpec((slot_count, head_dim), lambda h: (0, h)),
        out_shape=jax.ShapeDtypeStruct((slot_count, features), jnp.float32),
    )(projected, events, events, half_bias, live)


def shards(
    cand_x, cand_req, hist_len, block_place, kv_store, store_bucket, w_proj, w_out, time_bias
):
    axes = ("req", "cache")
    devices = lax.axis_size(axes)
    row_count = cand_x.shape[0]
    features = cand_x.shape[1]
    head_count = time_bias.shape[0]
    head_dim = features // head_count
    bucket_count = time_bias.shape[1]
    per_owner = kv_store.shape[2]
    block_ev = kv_store.shape[3]
    capacity = max(2, 2 * row_count // devices)
    event_count = devices * per_owner * block_ev

    target = cand_req[:, 0]
    onehot = (target[:, None] == jnp.arange(devices, dtype=jnp.int32)[None, :]).astype(jnp.int32)
    earlier = jnp.cumsum(onehot, axis=0) - onehot
    slot_rank = jnp.sum(earlier * onehot, axis=1)
    flat_slot = target * capacity + slot_rank
    empty = jnp.zeros((devices * capacity, features), cand_x.dtype)
    slotted = empty.at[flat_slot].set(cand_x).reshape(devices, capacity, features)
    rows_per = per_owner * block_ev
    bucket_lanes = rows_per // capacity
    bucket_send = store_bucket.reshape(devices, capacity, bucket_lanes).astype(cand_x.dtype)
    bucket_send = jnp.pad(bucket_send, ((0, 0), (0, 0), (0, 128 - bucket_lanes)))
    send = jnp.concatenate([slotted, bucket_send], axis=2)
    received = lax.all_to_all(send, axes, split_axis=0, concat_axis=0, tiled=True)
    received, kv_store = lax.optimization_barrier((received, kv_store))
    arrived = lax.all_to_all(kv_store, axes, split_axis=1, concat_axis=0, tiled=True)
    events = arrived.reshape(event_count, 2 * features)
    senders = received.shape[0]
    flat_rows = received[:, :, :features].reshape(senders * capacity, features)
    buckets = received[:, :, features : features + bucket_lanes].astype(jnp.int32).reshape(event_count)

    places = block_place[0]
    block_count = places.shape[0]
    block_ids = jnp.arange(block_count, dtype=jnp.int32)
    match = (places[:, None] == block_ids[None, :]).astype(jnp.int32)
    block_of_place = jnp.sum(match * block_ids[:, None], axis=0)
    position = (
        block_of_place[:, None] * block_ev + jnp.arange(block_ev, dtype=jnp.int32)[None, :]
    ).reshape(event_count, 1)
    live = (position < hist_len[0]).astype(jnp.float32)
    bucket_table = (buckets[None, :] == jnp.arange(bucket_count, dtype=jnp.int32)[:, None]).astype(
        jnp.float32
    )
    half_bias = 0.5 * jnp.dot(time_bias, bucket_table, precision=lax.Precision.HIGHEST)
    half_scale = 0.5 / math.sqrt(head_dim)

    projected = prepare(flat_rows, w_proj)
    slot_count = projected.shape[0]
    gate_u = projected[:, :features]
    attended = attend(projected, events, half_bias, live, head_count, head_dim, half_scale)
    hidden = (layer_norm(attended) * gate_u.astype(jnp.float32)).astype(jnp.bfloat16)
    update = (
        jnp.dot(hidden, w_out, preferred_element_type=jnp.float32)
        .astype(jnp.bfloat16)
        .reshape(senders, capacity, features)
    )
    returned = lax.all_to_all(update, axes, split_axis=0, concat_axis=0, tiled=True)
    update = returned.reshape(devices * capacity, features)[flat_slot]
    return (cand_x.astype(jnp.float32) + update.astype(jnp.float32)).astype(jnp.bfloat16)


def solution(mesh):
    placed = (
        P(("req", "cache"), None),
        P(("req", "cache"), None),
        P(("req", "cache")),
        P(("req", "cache"), None),
        P(("req", "cache"), None, None, None, None),
        P(("req", "cache"), None, None, None),
        P(),
        P(),
        P(),
    )
    return jax.shard_map(
        shards, mesh=mesh, in_specs=placed, out_specs=P(("req", "cache"), None), check_vma=False
    )
```

```python
import functools
import math

import jax
import jax.numpy as jnp
from jax import lax
from jax.experimental import pallas as pl
from jax.experimental.pallas import tpu as pltpu
from jax.sharding import PartitionSpec as P


def layer_norm(values):
    average = jnp.mean(values, axis=-1, keepdims=True)
    centred = values - average
    spread = jnp.mean(centred * centred, axis=-1, keepdims=True)
    return centred * lax.rsqrt(spread + 1e-05)


def prepare(inputs, w_proj):
    normed = layer_norm(inputs.astype(jnp.float32)).astype(jnp.bfloat16)
    return jax.nn.silu(jnp.dot(normed, w_proj, preferred_element_type=jnp.float32)).astype(
        jnp.bfloat16
    )


def attend_kernel(q_ref, k_ref, v_ref, bias_ref, live_ref, o_ref, *, half_scale, chunk):
    head = pl.program_id(0)
    query = q_ref[...]
    bias_row = bias_ref[pl.ds(head, 1), :]
    event_count = k_ref.shape[0]
    acc = jnp.zeros(o_ref.shape, jnp.float32)
    for c in range(event_count // chunk):
        lo = c * chunk
        key = k_ref[pl.ds(lo, chunk), :]
        value = v_ref[pl.ds(lo, chunk), :]
        value = jnp.where(live_ref[pl.ds(lo, chunk), :] > 0.0, value, jnp.zeros_like(value))
        scores = lax.dot_general(
            query, key, (((1,), (1,)), ((), ())), preferred_element_type=jnp.float32
        )
        half = scores * half_scale + bias_row[:, lo : lo + chunk]
        weight = (half + half * jnp.tanh(half)).astype(jnp.bfloat16)
        acc = acc + jnp.dot(weight, value, preferred_element_type=jnp.float32)
    o_ref[...] = acc


def attend(projected, events, half_bias, live, head_count, head_dim, half_scale):
    slot_count = projected.shape[0]
    event_count = events.shape[0]
    features = head_count * head_dim
    chunk = 512 if event_count % 512 == 0 else event_count
    kernel = functools.partial(attend_kernel, half_scale=half_scale, chunk=chunk)
    return pl.pallas_call(
        kernel,
        grid=(head_count,),
        in_specs=[
            pl.BlockSpec((slot_count, head_dim), lambda h: (0, head_count + h)),
            pl.BlockSpec((event_count, head_dim), lambda h: (0, h)),
            pl.BlockSpec((event_count, head_dim), lambda h: (0, head_count + h)),
            pl.BlockSpec(half_bias.shape, lambda h: (0, 0)),
            pl.BlockSpec(live.shape, lambda h: (0, 0)),
        ],
        out_specs=pl.BlockSpec((slot_count, head_dim), lambda h: (0, h)),
        out_shape=jax.ShapeDtypeStruct((slot_count, features), jnp.float32),
    )(projected, events, events, half_bias, live)


def finish_kernel(a_ref, g_ref, w_ref, o_ref):
    attended = a_ref[...]
    average = jnp.mean(attended, axis=-1, keepdims=True)
    centred = attended - average
    spread = jnp.mean(centred * centred, axis=-1, keepdims=True)
    normal = centred * lax.rsqrt(spread + 1e-05)
    hidden = (normal * g_ref[...].astype(jnp.float32)).astype(jnp.bfloat16)
    o_ref[...] = jnp.dot(hidden, w_ref[...], preferred_element_type=jnp.float32).astype(o_ref.dtype)


def finish(attended, projected, w_out):
    slot_count, features = attended.shape
    tile = 256 if slot_count % 256 == 0 else slot_count
    return pl.pallas_call(
        finish_kernel,
        grid=(slot_count // tile,),
        in_specs=[
            pl.BlockSpec((tile, features), lambda i: (i, 0)),
            pl.BlockSpec((tile, features), lambda i: (i, 0)),
            pl.BlockSpec(w_out.shape, lambda i: (0, 0)),
        ],
        out_specs=pl.BlockSpec((tile, w_out.shape[1]), lambda i: (i, 0)),
        out_shape=jax.ShapeDtypeStruct((slot_count, w_out.shape[1]), jnp.bfloat16),
    )(attended, projected, w_out)


def shards(
    cand_x, cand_req, hist_len, block_place, kv_store, store_bucket, w_proj, w_out, time_bias
):
    axes = ("req", "cache")
    devices = lax.axis_size(axes)
    row_count = cand_x.shape[0]
    features = cand_x.shape[1]
    head_count = time_bias.shape[0]
    head_dim = features // head_count
    bucket_count = time_bias.shape[1]
    per_owner = kv_store.shape[2]
    block_ev = kv_store.shape[3]
    capacity = max(2, 2 * row_count // devices)
    event_count = devices * per_owner * block_ev

    target = cand_req[:, 0]
    onehot = (target[:, None] == jnp.arange(devices, dtype=jnp.int32)[None, :]).astype(jnp.int32)
    earlier = jnp.cumsum(onehot, axis=0) - onehot
    slot_rank = jnp.sum(earlier * onehot, axis=1)
    flat_slot = target * capacity + slot_rank
    slot_ids = jnp.arange(devices * capacity, dtype=jnp.int32)
    slot_table = (flat_slot[:, None] == slot_ids[None, :]).astype(cand_x.dtype)
    slotted = lax.dot_general(
        slot_table, cand_x, (((0,), (0,)), ((), ())), preferred_element_type=jnp.float32
    )
    slotted = slotted.astype(cand_x.dtype).reshape(devices, capacity, features)
    rows_per = per_owner * block_ev
    bucket_lanes = rows_per // capacity
    bucket_send = store_bucket.reshape(devices, capacity, bucket_lanes).astype(cand_x.dtype)
    bucket_send = jnp.pad(bucket_send, ((0, 0), (0, 0), (0, 128 - bucket_lanes)))
    send = jnp.concatenate([slotted, bucket_send], axis=2)
    received = lax.all_to_all(send, axes, split_axis=0, concat_axis=0, tiled=True)
    received, kv_store = lax.optimization_barrier((received, kv_store))
    arrived = lax.all_to_all(kv_store, axes, split_axis=1, concat_axis=0, tiled=True)
    events = arrived.reshape(event_count, 2 * features)
    senders = received.shape[0]
    flat_rows = received[:, :, :features].reshape(senders * capacity, features)
    buckets = received[:, :, features : features + bucket_lanes].astype(jnp.int32).reshape(event_count)

    places = block_place[0]
    block_count = places.shape[0]
    block_ids = jnp.arange(block_count, dtype=jnp.int32)
    match = (places[:, None] == block_ids[None, :]).astype(jnp.int32)
    block_of_place = jnp.sum(match * block_ids[:, None], axis=0)
    position = (
        block_of_place[:, None] * block_ev + jnp.arange(block_ev, dtype=jnp.int32)[None, :]
    ).reshape(event_count, 1)
    live = (position < hist_len[0]).astype(jnp.float32)
    bucket_table = (buckets[None, :] == jnp.arange(bucket_count, dtype=jnp.int32)[:, None]).astype(
        jnp.float32
    )
    half_bias = 0.5 * jnp.dot(time_bias, bucket_table, precision=lax.Precision.HIGHEST)
    half_scale = 0.5 / math.sqrt(head_dim)

    projected = prepare(flat_rows, w_proj)
    slot_count = projected.shape[0]
    attended = attend(projected, events, half_bias, live, head_count, head_dim, half_scale)
    update = finish(attended, projected, w_out).reshape(senders, capacity, features)
    returned = lax.all_to_all(update, axes, split_axis=0, concat_axis=0, tiled=True)
    picked = jnp.dot(
        slot_table, returned.reshape(devices * capacity, features), preferred_element_type=jnp.float32
    )
    return (cand_x.astype(jnp.float32) + picked).astype(jnp.bfloat16)


def solution(mesh):
    placed = (
        P(("req", "cache"), None),
        P(("req", "cache"), None),
        P(("req", "cache")),
        P(("req", "cache"), None),
        P(("req", "cache"), None, None, None, None),
        P(("req", "cache"), None, None, None),
        P(),
        P(),
        P(),
    )
    return jax.shard_map(
        shards, mesh=mesh, in_specs=placed, out_specs=P(("req", "cache"), None), check_vma=False
    )
```

```python
import functools
import math

import jax
import jax.numpy as jnp
from jax import lax
from jax.experimental import pallas as pl
from jax.experimental.pallas import tpu as pltpu
from jax.sharding import PartitionSpec as P


def layer_norm(values):
    average = jnp.mean(values, axis=-1, keepdims=True)
    centred = values - average
    spread = jnp.mean(centred * centred, axis=-1, keepdims=True)
    return centred * lax.rsqrt(spread + 1e-05)


def prepare(inputs, w_proj):
    normed = layer_norm(inputs.astype(jnp.float32)).astype(jnp.bfloat16)
    return jax.nn.silu(jnp.dot(normed, w_proj, preferred_element_type=jnp.float32)).astype(
        jnp.bfloat16
    )


def attend_kernel(q_ref, k_ref, v_ref, bias_ref, live_ref, o_ref, *, half_scale, chunk, first):
    head = pl.program_id(0) + first
    query = q_ref[...]
    bias_row = bias_ref[pl.ds(head, 1), :]
    event_count = k_ref.shape[0]
    acc = jnp.zeros(o_ref.shape, jnp.float32)
    for c in range(event_count // chunk):
        lo = c * chunk
        key = k_ref[pl.ds(lo, chunk), :]
        value = v_ref[pl.ds(lo, chunk), :]
        value = jnp.where(live_ref[pl.ds(lo, chunk), :] > 0.0, value, jnp.zeros_like(value))
        scores = lax.dot_general(
            query, key, (((1,), (1,)), ((), ())), preferred_element_type=jnp.float32
        )
        half = scores * half_scale + bias_row[:, lo : lo + chunk]
        weight = (half + half * jnp.tanh(half)).astype(jnp.bfloat16)
        acc = acc + jnp.dot(weight, value, preferred_element_type=jnp.float32)
    o_ref[...] = acc


def attend(projected, events, half_bias, live, head_count, head_dim, half_scale, first):
    slot_count = projected.shape[0]
    event_count = events.shape[0]
    total_heads = half_bias.shape[0]
    chunk = 512 if event_count % 512 == 0 else event_count
    kernel = functools.partial(attend_kernel, half_scale=half_scale, chunk=chunk, first=first)
    return pl.pallas_call(
        kernel,
        grid=(head_count,),
        in_specs=[
            pl.BlockSpec((slot_count, head_dim), lambda h: (0, total_heads + first + h)),
            pl.BlockSpec((event_count, head_dim), lambda h: (0, h)),
            pl.BlockSpec((event_count, head_dim), lambda h: (0, head_count + h)),
            pl.BlockSpec(half_bias.shape, lambda h: (0, 0)),
            pl.BlockSpec(live.shape, lambda h: (0, 0)),
        ],
        out_specs=pl.BlockSpec((slot_count, head_dim), lambda h: (0, h)),
        out_shape=jax.ShapeDtypeStruct((slot_count, head_count * head_dim), jnp.float32),
    )(projected, events, events, half_bias, live)


def finish_kernel(a_ref, b_ref, g_ref, w_ref, o_ref):
    attended = jnp.concatenate([a_ref[...], b_ref[...]], axis=1)
    average = jnp.mean(attended, axis=-1, keepdims=True)
    centred = attended - average
    spread = jnp.mean(centred * centred, axis=-1, keepdims=True)
    normal = centred * lax.rsqrt(spread + 1e-05)
    hidden = (normal * g_ref[...].astype(jnp.float32)).astype(jnp.bfloat16)
    o_ref[...] = jnp.dot(hidden, w_ref[...], preferred_element_type=jnp.float32).astype(o_ref.dtype)


def finish(first_half, second_half, projected, w_out):
    slot_count, half = first_half.shape
    features = 2 * half
    tile = 256 if slot_count % 256 == 0 else slot_count
    return pl.pallas_call(
        finish_kernel,
        grid=(slot_count // tile,),
        in_specs=[
            pl.BlockSpec((tile, half), lambda i: (i, 0)),
            pl.BlockSpec((tile, half), lambda i: (i, 0)),
            pl.BlockSpec((tile, features), lambda i: (i, 0)),
            pl.BlockSpec(w_out.shape, lambda i: (0, 0)),
        ],
        out_specs=pl.BlockSpec((tile, w_out.shape[1]), lambda i: (i, 0)),
        out_shape=jax.ShapeDtypeStruct((slot_count, w_out.shape[1]), jnp.bfloat16),
    )(first_half, second_half, projected, w_out)


def shards(
    cand_x, cand_req, hist_len, block_place, kv_store, store_bucket, w_proj, w_out, time_bias
):
    axes = ("req", "cache")
    devices = lax.axis_size(axes)
    row_count = cand_x.shape[0]
    features = cand_x.shape[1]
    head_count = time_bias.shape[0]
    head_dim = features // head_count
    bucket_count = time_bias.shape[1]
    per_owner = kv_store.shape[2]
    block_ev = kv_store.shape[3]
    capacity = max(2, 2 * row_count // devices)
    event_count = devices * per_owner * block_ev

    target = cand_req[:, 0]
    onehot = (target[:, None] == jnp.arange(devices, dtype=jnp.int32)[None, :]).astype(jnp.int32)
    earlier = jnp.cumsum(onehot, axis=0) - onehot
    slot_rank = jnp.sum(earlier * onehot, axis=1)
    flat_slot = target * capacity + slot_rank
    slot_ids = jnp.arange(devices * capacity, dtype=jnp.int32)
    slot_table = (flat_slot[:, None] == slot_ids[None, :]).astype(cand_x.dtype)
    slotted = lax.dot_general(
        slot_table, cand_x, (((0,), (0,)), ((), ())), preferred_element_type=jnp.float32
    )
    slotted = slotted.astype(cand_x.dtype).reshape(devices, capacity, features)
    rows_per = per_owner * block_ev
    bucket_lanes = rows_per // capacity
    bucket_send = store_bucket.reshape(devices, capacity, bucket_lanes).astype(cand_x.dtype)
    bucket_send = jnp.pad(bucket_send, ((0, 0), (0, 0), (0, 128 - bucket_lanes)))
    send = jnp.concatenate([slotted, bucket_send], axis=2)
    half_heads = head_count // 2
    split = half_heads * head_dim
    kv_first = jnp.concatenate(
        [kv_store[..., :split], kv_store[..., features : features + split]], axis=-1
    )
    kv_second = jnp.concatenate(
        [kv_store[..., split:features], kv_store[..., features + split :]], axis=-1
    )
    arrived_first = lax.all_to_all(kv_first, axes, split_axis=1, concat_axis=0, tiled=True)
    arrived_first, send = lax.optimization_barrier((arrived_first, send))
    received = lax.all_to_all(send, axes, split_axis=0, concat_axis=0, tiled=True)
    received, kv_second = lax.optimization_barrier((received, kv_second))
    arrived_second = lax.all_to_all(kv_second, axes, split_axis=1, concat_axis=0, tiled=True)
    events_first = arrived_first.reshape(event_count, features)
    events_second = arrived_second.reshape(event_count, features)
    senders = received.shape[0]
    flat_rows = received[:, :, :features].reshape(senders * capacity, features)
    buckets = received[:, :, features : features + bucket_lanes].astype(jnp.int32).reshape(event_count)

    places = block_place[0]
    block_count = places.shape[0]
    block_ids = jnp.arange(block_count, dtype=jnp.int32)
    match = (places[:, None] == block_ids[None, :]).astype(jnp.int32)
    block_of_place = jnp.sum(match * block_ids[:, None], axis=0)
    position = (
        block_of_place[:, None] * block_ev + jnp.arange(block_ev, dtype=jnp.int32)[None, :]
    ).reshape(event_count, 1)
    live = (position < hist_len[0]).astype(jnp.float32)
    bucket_table = (buckets[None, :] == jnp.arange(bucket_count, dtype=jnp.int32)[:, None]).astype(
        jnp.float32
    )
    half_bias = 0.5 * jnp.dot(time_bias, bucket_table, precision=lax.Precision.HIGHEST)
    half_scale = 0.5 / math.sqrt(head_dim)

    projected = prepare(flat_rows, w_proj)
    slot_count = projected.shape[0]
    attended_first = attend(
        projected, events_first, half_bias, live, half_heads, head_dim, half_scale, 0
    )
    attended_second = attend(
        projected, events_second, half_bias, live, half_heads, head_dim, half_scale, half_heads
    )
    update = finish(attended_first, attended_second, projected, w_out)
    update = update.reshape(senders, capacity, features)
    returned = lax.all_to_all(update, axes, split_axis=0, concat_axis=0, tiled=True)
    picked = jnp.dot(
        slot_table, returned.reshape(devices * capacity, features), preferred_element_type=jnp.float32
    )
    return (cand_x.astype(jnp.float32) + picked).astype(jnp.bfloat16)


def solution(mesh):
    placed = (
        P(("req", "cache"), None),
        P(("req", "cache"), None),
        P(("req", "cache")),
        P(("req", "cache"), None),
        P(("req", "cache"), None, None, None, None),
        P(("req", "cache"), None, None, None),
        P(),
        P(),
        P(),
    )
    return jax.shard_map(
        shards, mesh=mesh, in_specs=placed, out_specs=P(("req", "cache"), None), check_vma=False
    )
```

```python
import functools
import math

import jax
import jax.numpy as jnp
from jax import lax
from jax.experimental import pallas as pl
from jax.experimental.pallas import tpu as pltpu
from jax.sharding import PartitionSpec as P


def layer_norm(values):
    average = jnp.mean(values, axis=-1, keepdims=True)
    centred = values - average
    spread = jnp.mean(centred * centred, axis=-1, keepdims=True)
    return centred * lax.rsqrt(spread + 1e-05)


def prepare(inputs, w_proj):
    normed = layer_norm(inputs.astype(jnp.float32)).astype(jnp.bfloat16)
    return jax.nn.silu(jnp.dot(normed, w_proj, preferred_element_type=jnp.float32)).astype(
        jnp.bfloat16
    )


def attend_kernel(q_ref, k_ref, v_ref, bias_ref, live_ref, o_ref, *, half_scale, chunk, first):
    head = pl.program_id(0) + first
    query = q_ref[...]
    bias_row = bias_ref[pl.ds(head, 1), :]
    event_count = k_ref.shape[0]
    acc = jnp.zeros(o_ref.shape, jnp.float32)
    for c in range(event_count // chunk):
        lo = c * chunk
        key = k_ref[pl.ds(lo, chunk), :]
        value = v_ref[pl.ds(lo, chunk), :]
        value = jnp.where(live_ref[pl.ds(lo, chunk), :] > 0.0, value, jnp.zeros_like(value))
        scores = lax.dot_general(
            query, key, (((1,), (1,)), ((), ())), preferred_element_type=jnp.float32
        )
        half = scores * half_scale + bias_row[:, lo : lo + chunk]
        weight = (half + half * jnp.tanh(half)).astype(jnp.bfloat16)
        acc = acc + jnp.dot(weight, value, preferred_element_type=jnp.float32)
    o_ref[...] = acc


def attend(projected, events, half_bias, live, head_count, head_dim, half_scale, first):
    slot_count = projected.shape[0]
    event_count = events.shape[0]
    total_heads = half_bias.shape[0]
    chunk = 512 if event_count % 512 == 0 else event_count
    kernel = functools.partial(attend_kernel, half_scale=half_scale, chunk=chunk, first=first)
    return pl.pallas_call(
        kernel,
        grid=(head_count,),
        in_specs=[
            pl.BlockSpec((slot_count, head_dim), lambda h: (0, total_heads + first + h)),
            pl.BlockSpec((event_count, head_dim), lambda h: (0, h)),
            pl.BlockSpec((event_count, head_dim), lambda h: (0, head_count + h)),
            pl.BlockSpec(half_bias.shape, lambda h: (0, 0)),
            pl.BlockSpec(live.shape, lambda h: (0, 0)),
        ],
        out_specs=pl.BlockSpec((slot_count, head_dim), lambda h: (0, h)),
        out_shape=jax.ShapeDtypeStruct((slot_count, head_count * head_dim), jnp.float32),
    )(projected, events, events, half_bias, live)


def finish_kernel(a_ref, b_ref, g_ref, w_ref, o_ref):
    attended = jnp.concatenate([a_ref[...], b_ref[...]], axis=1)
    average = jnp.mean(attended, axis=-1, keepdims=True)
    centred = attended - average
    spread = jnp.mean(centred * centred, axis=-1, keepdims=True)
    normal = centred * lax.rsqrt(spread + 1e-05)
    hidden = (normal * g_ref[...].astype(jnp.float32)).astype(jnp.bfloat16)
    o_ref[...] = jnp.dot(hidden, w_ref[...], preferred_element_type=jnp.float32).astype(o_ref.dtype)


def finish(first_half, second_half, projected, w_out):
    slot_count, half = first_half.shape
    features = 2 * half
    tile = 256 if slot_count % 256 == 0 else slot_count
    return pl.pallas_call(
        finish_kernel,
        grid=(slot_count // tile,),
        in_specs=[
            pl.BlockSpec((tile, half), lambda i: (i, 0)),
            pl.BlockSpec((tile, half), lambda i: (i, 0)),
            pl.BlockSpec((tile, features), lambda i: (i, 0)),
            pl.BlockSpec(w_out.shape, lambda i: (0, 0)),
        ],
        out_specs=pl.BlockSpec((tile, w_out.shape[1]), lambda i: (i, 0)),
        out_shape=jax.ShapeDtypeStruct((slot_count, w_out.shape[1]), jnp.bfloat16),
    )(first_half, second_half, projected, w_out)


def shards(
    cand_x, cand_req, hist_len, block_place, kv_store, store_bucket, w_proj, w_out, time_bias
):
    axes = ("req", "cache")
    devices = lax.axis_size(axes)
    row_count = cand_x.shape[0]
    features = cand_x.shape[1]
    head_count = time_bias.shape[0]
    head_dim = features // head_count
    bucket_count = time_bias.shape[1]
    per_owner = kv_store.shape[2]
    block_ev = kv_store.shape[3]
    capacity = max(2, 2 * row_count // devices)
    event_count = devices * per_owner * block_ev

    target = cand_req[:, 0]
    onehot = (target[:, None] == jnp.arange(devices, dtype=jnp.int32)[None, :]).astype(jnp.int32)
    earlier = jnp.cumsum(onehot, axis=0) - onehot
    slot_rank = jnp.sum(earlier * onehot, axis=1)
    flat_slot = target * capacity + slot_rank
    slot_ids = jnp.arange(devices * capacity, dtype=jnp.int32)
    slot_table = (flat_slot[:, None] == slot_ids[None, :]).astype(cand_x.dtype)
    slotted = lax.dot_general(
        slot_table, cand_x, (((0,), (0,)), ((), ())), preferred_element_type=jnp.float32
    )
    slotted = slotted.astype(cand_x.dtype).reshape(devices, capacity, features)
    rows_per = per_owner * block_ev
    half_heads = head_count // 2
    split = half_heads * head_dim
    kv_first = jnp.concatenate(
        [kv_store[..., :split], kv_store[..., features : features + split]], axis=-1
    ).reshape(devices, rows_per, 2 * split)
    kv_second = jnp.concatenate(
        [kv_store[..., split:features], kv_store[..., features + split :]], axis=-1
    )
    query_width = capacity * features // rows_per
    bucket_send = store_bucket.reshape(devices, rows_per, 1).astype(cand_x.dtype)
    bucket_send = jnp.pad(bucket_send, ((0, 0), (0, 0), (0, 127)))
    send = jnp.concatenate(
        [kv_first, slotted.reshape(devices, rows_per, query_width), bucket_send], axis=2
    )
    received = lax.all_to_all(send, axes, split_axis=0, concat_axis=0, tiled=True)
    received, kv_second = lax.optimization_barrier((received, kv_second))
    arrived_second = lax.all_to_all(kv_second, axes, split_axis=1, concat_axis=0, tiled=True)
    senders = received.shape[0]
    width = received.shape[2]
    events_first = received.reshape(event_count, width)
    events_second = arrived_second.reshape(event_count, features)
    flat_rows = received[:, :, 2 * split : 2 * split + query_width].reshape(
        senders * capacity, features
    )
    buckets = received[:, :, 2 * split + query_width].astype(jnp.int32).reshape(event_count)

    places = block_place[0]
    block_count = places.shape[0]
    block_ids = jnp.arange(block_count, dtype=jnp.int32)
    match = (places[:, None] == block_ids[None, :]).astype(jnp.int32)
    block_of_place = jnp.sum(match * block_ids[:, None], axis=0)
    position = (
        block_of_place[:, None] * block_ev + jnp.arange(block_ev, dtype=jnp.int32)[None, :]
    ).reshape(event_count, 1)
    live = (position < hist_len[0]).astype(jnp.float32)
    bucket_table = (buckets[None, :] == jnp.arange(bucket_count, dtype=jnp.int32)[:, None]).astype(
        jnp.float32
    )
    half_bias = 0.5 * jnp.dot(time_bias, bucket_table, precision=lax.Precision.HIGHEST)
    half_scale = 0.5 / math.sqrt(head_dim)

    projected = prepare(flat_rows, w_proj)
    slot_count = projected.shape[0]
    attended_first = attend(
        projected, events_first, half_bias, live, half_heads, head_dim, half_scale, 0
    )
    attended_second = attend(
        projected, events_second, half_bias, live, half_heads, head_dim, half_scale, half_heads
    )
    update = finish(attended_first, attended_second, projected, w_out)
    update = update.reshape(senders, capacity, features)
    returned = lax.all_to_all(update, axes, split_axis=0, concat_axis=0, tiled=True)
    picked = jnp.dot(
        slot_table, returned.reshape(devices * capacity, features), preferred_element_type=jnp.float32
    )
    return (cand_x.astype(jnp.float32) + picked).astype(jnp.bfloat16)


def solution(mesh):
    placed = (
        P(("req", "cache"), None),
        P(("req", "cache"), None),
        P(("req", "cache")),
        P(("req", "cache"), None),
        P(("req", "cache"), None, None, None, None),
        P(("req", "cache"), None, None, None),
        P(),
        P(),
        P(),
    )
    return jax.shard_map(
        shards, mesh=mesh, in_specs=placed, out_specs=P(("req", "cache"), None), check_vma=False
    )
```

```python
import functools
import math

import jax
import jax.numpy as jnp
from jax import lax
from jax.experimental import pallas as pl
from jax.experimental.pallas import tpu as pltpu
from jax.sharding import PartitionSpec as P


def layer_norm(values):
    average = jnp.mean(values, axis=-1, keepdims=True)
    centred = values - average
    spread = jnp.mean(centred * centred, axis=-1, keepdims=True)
    return centred * lax.rsqrt(spread + 1e-05)


def prepare(inputs, w_proj):
    normed = layer_norm(inputs.astype(jnp.float32)).astype(jnp.bfloat16)
    return jax.nn.silu(jnp.dot(normed, w_proj, preferred_element_type=jnp.float32)).astype(
        jnp.bfloat16
    )


def attend_kernel(q_ref, k_ref, v_ref, bias_ref, live_ref, o_ref, *, half_scale, chunk, first):
    head = pl.program_id(0) + first
    query = q_ref[...]
    bias_row = bias_ref[pl.ds(head, 1), :]
    event_count = k_ref.shape[0]
    acc = jnp.zeros(o_ref.shape, jnp.float32)
    for c in range(event_count // chunk):
        lo = c * chunk
        key = k_ref[pl.ds(lo, chunk), :]
        value = v_ref[pl.ds(lo, chunk), :]
        value = jnp.where(live_ref[pl.ds(lo, chunk), :] > 0.0, value, jnp.zeros_like(value))
        scores = lax.dot_general(
            query, key, (((1,), (1,)), ((), ())), preferred_element_type=jnp.float32
        )
        half = scores * half_scale + bias_row[:, lo : lo + chunk]
        weight = (half + half * jnp.tanh(half)).astype(jnp.bfloat16)
        acc = acc + jnp.dot(weight, value, preferred_element_type=jnp.float32)
    o_ref[...] = acc


def attend(projected, events, half_bias, live, head_count, head_dim, half_scale, first):
    slot_count = projected.shape[0]
    event_count = events.shape[0]
    total_heads = half_bias.shape[0]
    chunk = 512 if event_count % 512 == 0 else event_count
    kernel = functools.partial(attend_kernel, half_scale=half_scale, chunk=chunk, first=first)
    return pl.pallas_call(
        kernel,
        grid=(head_count,),
        in_specs=[
            pl.BlockSpec((slot_count, head_dim), lambda h: (0, total_heads + first + h)),
            pl.BlockSpec((event_count, head_dim), lambda h: (0, h)),
            pl.BlockSpec((event_count, head_dim), lambda h: (0, head_count + h)),
            pl.BlockSpec(half_bias.shape, lambda h: (0, 0)),
            pl.BlockSpec(live.shape, lambda h: (0, 0)),
        ],
        out_specs=pl.BlockSpec((slot_count, head_dim), lambda h: (0, h)),
        out_shape=jax.ShapeDtypeStruct((slot_count, head_count * head_dim), jnp.float32),
    )(projected, events, events, half_bias, live)


def finish_kernel(a_ref, b_ref, g_ref, w_ref, o_ref):
    attended = jnp.concatenate([a_ref[...], b_ref[...]], axis=1)
    average = jnp.mean(attended, axis=-1, keepdims=True)
    centred = attended - average
    spread = jnp.mean(centred * centred, axis=-1, keepdims=True)
    normal = centred * lax.rsqrt(spread + 1e-05)
    hidden = (normal * g_ref[...].astype(jnp.float32)).astype(jnp.bfloat16)
    o_ref[...] = jnp.dot(hidden, w_ref[...], preferred_element_type=jnp.float32).astype(o_ref.dtype)


def finish(first_half, second_half, projected, w_out):
    slot_count, half = first_half.shape
    features = 2 * half
    tile = 256 if slot_count % 256 == 0 else slot_count
    return pl.pallas_call(
        finish_kernel,
        grid=(slot_count // tile,),
        in_specs=[
            pl.BlockSpec((tile, half), lambda i: (i, 0)),
            pl.BlockSpec((tile, half), lambda i: (i, 0)),
            pl.BlockSpec((tile, features), lambda i: (i, 0)),
            pl.BlockSpec(w_out.shape, lambda i: (0, 0)),
        ],
        out_specs=pl.BlockSpec((tile, w_out.shape[1]), lambda i: (i, 0)),
        out_shape=jax.ShapeDtypeStruct((slot_count, w_out.shape[1]), jnp.bfloat16),
    )(first_half, second_half, projected, w_out)


def shards(
    cand_x, cand_req, hist_len, block_place, kv_store, store_bucket, w_proj, w_out, time_bias
):
    axes = ("req", "cache")
    devices = lax.axis_size(axes)
    row_count = cand_x.shape[0]
    features = cand_x.shape[1]
    head_count = time_bias.shape[0]
    head_dim = features // head_count
    bucket_count = time_bias.shape[1]
    per_owner = kv_store.shape[2]
    block_ev = kv_store.shape[3]
    capacity = max(2, 2 * row_count // devices)
    event_count = devices * per_owner * block_ev

    target = cand_req[:, 0]
    onehot = (target[:, None] == jnp.arange(devices, dtype=jnp.int32)[None, :]).astype(jnp.int32)
    earlier = jnp.cumsum(onehot, axis=0) - onehot
    slot_rank = jnp.sum(earlier * onehot, axis=1)
    flat_slot = target * capacity + slot_rank
    slot_ids = jnp.arange(devices * capacity, dtype=jnp.int32)
    slot_table = (flat_slot[:, None] == slot_ids[None, :]).astype(cand_x.dtype)
    slotted = lax.dot_general(
        slot_table, cand_x, (((0,), (0,)), ((), ())), preferred_element_type=jnp.float32
    )
    slotted = slotted.astype(cand_x.dtype).reshape(devices, capacity, features)
    rows_per = per_owner * block_ev
    bucket_lanes = rows_per // capacity
    bucket_send = store_bucket.reshape(devices, capacity, bucket_lanes).astype(cand_x.dtype)
    bucket_send = jnp.pad(bucket_send, ((0, 0), (0, 0), (0, 128 - bucket_lanes)))
    send = jnp.concatenate([slotted, bucket_send], axis=2)
    half_heads = head_count // 2
    split = half_heads * head_dim
    kv_first = jnp.concatenate(
        [kv_store[..., :split], kv_store[..., features : features + split]], axis=-1
    )
    kv_second = jnp.concatenate(
        [kv_store[..., split:features], kv_store[..., features + split :]], axis=-1
    )
    received = lax.all_to_all(send, axes, split_axis=0, concat_axis=0, tiled=True)
    received, kv_first = lax.optimization_barrier((received, kv_first))
    arrived_first = lax.all_to_all(kv_first, axes, split_axis=1, concat_axis=0, tiled=True)
    arrived_first, kv_second = lax.optimization_barrier((arrived_first, kv_second))
    arrived_second = lax.all_to_all(kv_second, axes, split_axis=1, concat_axis=0, tiled=True)
    events_first = arrived_first.reshape(event_count, features)
    events_second = arrived_second.reshape(event_count, features)
    senders = received.shape[0]
    flat_rows = received[:, :, :features].reshape(senders * capacity, features)
    buckets = received[:, :, features : features + bucket_lanes].astype(jnp.int32).reshape(event_count)

    places = block_place[0]
    block_count = places.shape[0]
    block_ids = jnp.arange(block_count, dtype=jnp.int32)
    match = (places[:, None] == block_ids[None, :]).astype(jnp.int32)
    block_of_place = jnp.sum(match * block_ids[:, None], axis=0)
    position = (
        block_of_place[:, None] * block_ev + jnp.arange(block_ev, dtype=jnp.int32)[None, :]
    ).reshape(event_count, 1)
    live = (position < hist_len[0]).astype(jnp.float32)
    bucket_table = (buckets[None, :] == jnp.arange(bucket_count, dtype=jnp.int32)[:, None]).astype(
        jnp.float32
    )
    half_bias = 0.5 * jnp.dot(time_bias, bucket_table, precision=lax.Precision.HIGHEST)
    half_scale = 0.5 / math.sqrt(head_dim)

    projected = prepare(flat_rows, w_proj)
    slot_count = projected.shape[0]
    attended_first = attend(
        projected, events_first, half_bias, live, half_heads, head_dim, half_scale, 0
    )
    attended_second = attend(
        projected, events_second, half_bias, live, half_heads, head_dim, half_scale, half_heads
    )
    update = finish(attended_first, attended_second, projected, w_out)
    update = update.reshape(senders, capacity, features)
    returned = lax.all_to_all(update, axes, split_axis=0, concat_axis=0, tiled=True)
    picked = jnp.dot(
        slot_table, returned.reshape(devices * capacity, features), preferred_element_type=jnp.float32
    )
    return (cand_x.astype(jnp.float32) + picked).astype(jnp.bfloat16)


def solution(mesh):
    placed = (
        P(("req", "cache"), None),
        P(("req", "cache"), None),
        P(("req", "cache")),
        P(("req", "cache"), None),
        P(("req", "cache"), None, None, None, None),
        P(("req", "cache"), None, None, None),
        P(),
        P(),
        P(),
    )
    return jax.shard_map(
        shards, mesh=mesh, in_specs=placed, out_specs=P(("req", "cache"), None), check_vma=False
    )
```

```python
import functools
import math

import jax
import jax.numpy as jnp
from jax import lax
from jax.experimental import pallas as pl
from jax.experimental.pallas import tpu as pltpu
from jax.sharding import PartitionSpec as P


def layer_norm(values):
    average = jnp.mean(values, axis=-1, keepdims=True)
    centred = values - average
    spread = jnp.mean(centred * centred, axis=-1, keepdims=True)
    return centred * lax.rsqrt(spread + 1e-05)


def prepare(inputs, w_proj):
    normed = layer_norm(inputs.astype(jnp.float32)).astype(jnp.bfloat16)
    return jax.nn.silu(jnp.dot(normed, w_proj, preferred_element_type=jnp.float32)).astype(
        jnp.bfloat16
    )


def attend_kernel(q_ref, k_ref, v_ref, bias_ref, live_ref, o_ref, *, half_scale, chunk, first):
    head = pl.program_id(0) + first
    query = q_ref[...]
    bias_row = bias_ref[pl.ds(head, 1), :]
    event_count = k_ref.shape[0]
    acc = jnp.zeros(o_ref.shape, jnp.float32)
    for c in range(event_count // chunk):
        lo = c * chunk
        key = k_ref[pl.ds(lo, chunk), :]
        value = v_ref[pl.ds(lo, chunk), :]
        value = jnp.where(live_ref[pl.ds(lo, chunk), :] > 0.0, value, jnp.zeros_like(value))
        scores = lax.dot_general(
            query, key, (((1,), (1,)), ((), ())), preferred_element_type=jnp.float32
        )
        half = scores * half_scale + bias_row[:, lo : lo + chunk]
        weight = (half + half * jnp.tanh(half)).astype(jnp.bfloat16)
        acc = acc + jnp.dot(weight, value, preferred_element_type=jnp.float32)
    o_ref[...] = acc


def attend(projected, events, half_bias, live, head_count, head_dim, half_scale, first):
    slot_count = projected.shape[0]
    event_count = events.shape[0]
    total_heads = half_bias.shape[0]
    chunk = 512 if event_count % 512 == 0 else event_count
    kernel = functools.partial(attend_kernel, half_scale=half_scale, chunk=chunk, first=first)
    return pl.pallas_call(
        kernel,
        grid=(head_count,),
        in_specs=[
            pl.BlockSpec((slot_count, head_dim), lambda h: (0, total_heads + first + h)),
            pl.BlockSpec((event_count, head_dim), lambda h: (0, h)),
            pl.BlockSpec((event_count, head_dim), lambda h: (0, head_count + h)),
            pl.BlockSpec(half_bias.shape, lambda h: (0, 0)),
            pl.BlockSpec(live.shape, lambda h: (0, 0)),
        ],
        out_specs=pl.BlockSpec((slot_count, head_dim), lambda h: (0, h)),
        out_shape=jax.ShapeDtypeStruct((slot_count, head_count * head_dim), jnp.float32),
    )(projected, events, events, half_bias, live)


def finish_kernel(a_ref, b_ref, g_ref, w_ref, o_ref):
    attended = jnp.concatenate([a_ref[...], b_ref[...]], axis=1)
    average = jnp.mean(attended, axis=-1, keepdims=True)
    centred = attended - average
    spread = jnp.mean(centred * centred, axis=-1, keepdims=True)
    normal = centred * lax.rsqrt(spread + 1e-05)
    hidden = (normal * g_ref[...].astype(jnp.float32)).astype(jnp.bfloat16)
    o_ref[...] = jnp.dot(hidden, w_ref[...], preferred_element_type=jnp.float32).astype(o_ref.dtype)


def finish(first_half, second_half, projected, w_out):
    slot_count, first_width = first_half.shape
    second_width = second_half.shape[1]
    features = first_width + second_width
    tile = 256 if slot_count % 256 == 0 else slot_count
    return pl.pallas_call(
        finish_kernel,
        grid=(slot_count // tile,),
        in_specs=[
            pl.BlockSpec((tile, first_width), lambda i: (i, 0)),
            pl.BlockSpec((tile, second_width), lambda i: (i, 0)),
            pl.BlockSpec((tile, features), lambda i: (i, 0)),
            pl.BlockSpec(w_out.shape, lambda i: (0, 0)),
        ],
        out_specs=pl.BlockSpec((tile, w_out.shape[1]), lambda i: (i, 0)),
        out_shape=jax.ShapeDtypeStruct((slot_count, w_out.shape[1]), jnp.bfloat16),
    )(first_half, second_half, projected, w_out)


def shards(
    cand_x, cand_req, hist_len, block_place, kv_store, store_bucket, w_proj, w_out, time_bias
):
    axes = ("req", "cache")
    devices = lax.axis_size(axes)
    row_count = cand_x.shape[0]
    features = cand_x.shape[1]
    head_count = time_bias.shape[0]
    head_dim = features // head_count
    bucket_count = time_bias.shape[1]
    per_owner = kv_store.shape[2]
    block_ev = kv_store.shape[3]
    capacity = max(2, 2 * row_count // devices)
    event_count = devices * per_owner * block_ev

    target = cand_req[:, 0]
    onehot = (target[:, None] == jnp.arange(devices, dtype=jnp.int32)[None, :]).astype(jnp.int32)
    earlier = jnp.cumsum(onehot, axis=0) - onehot
    slot_rank = jnp.sum(earlier * onehot, axis=1)
    flat_slot = target * capacity + slot_rank
    slot_ids = jnp.arange(devices * capacity, dtype=jnp.int32)
    slot_table = (flat_slot[:, None] == slot_ids[None, :]).astype(cand_x.dtype)
    slotted = lax.dot_general(
        slot_table, cand_x, (((0,), (0,)), ((), ())), preferred_element_type=jnp.float32
    )
    slotted = slotted.astype(cand_x.dtype).reshape(devices, capacity, features)
    rows_per = per_owner * block_ev
    bucket_lanes = rows_per // capacity
    bucket_send = store_bucket.reshape(devices, capacity, bucket_lanes).astype(cand_x.dtype)
    bucket_send = jnp.pad(bucket_send, ((0, 0), (0, 0), (0, 128 - bucket_lanes)))
    send = jnp.concatenate([slotted, bucket_send], axis=2)
    first_heads = head_count * 3 // 4
    split = first_heads * head_dim
    kv_first = jnp.concatenate(
        [kv_store[..., :split], kv_store[..., features : features + split]], axis=-1
    )
    kv_second = jnp.concatenate(
        [kv_store[..., split:features], kv_store[..., features + split :]], axis=-1
    )
    received = lax.all_to_all(send, axes, split_axis=0, concat_axis=0, tiled=True)
    received, kv_first = lax.optimization_barrier((received, kv_first))
    arrived_first = lax.all_to_all(kv_first, axes, split_axis=1, concat_axis=0, tiled=True)
    arrived_first, kv_second = lax.optimization_barrier((arrived_first, kv_second))
    arrived_second = lax.all_to_all(kv_second, axes, split_axis=1, concat_axis=0, tiled=True)
    events_first = arrived_first.reshape(event_count, 2 * split)
    events_second = arrived_second.reshape(event_count, 2 * (features - split))
    senders = received.shape[0]
    flat_rows = received[:, :, :features].reshape(senders * capacity, features)
    buckets = received[:, :, features : features + bucket_lanes].astype(jnp.int32).reshape(event_count)

    places = block_place[0]
    block_count = places.shape[0]
    block_ids = jnp.arange(block_count, dtype=jnp.int32)
    match = (places[:, None] == block_ids[None, :]).astype(jnp.int32)
    block_of_place = jnp.sum(match * block_ids[:, None], axis=0)
    position = (
        block_of_place[:, None] * block_ev + jnp.arange(block_ev, dtype=jnp.int32)[None, :]
    ).reshape(event_count, 1)
    live = (position < hist_len[0]).astype(jnp.float32)
    bucket_table = (buckets[None, :] == jnp.arange(bucket_count, dtype=jnp.int32)[:, None]).astype(
        jnp.float32
    )
    half_bias = 0.5 * jnp.dot(time_bias, bucket_table, precision=lax.Precision.HIGHEST)
    half_scale = 0.5 / math.sqrt(head_dim)

    projected = prepare(flat_rows, w_proj)
    slot_count = projected.shape[0]
    attended_first = attend(
        projected, events_first, half_bias, live, first_heads, head_dim, half_scale, 0
    )
    second_heads = head_count - first_heads
    attended_second = attend(
        projected, events_second, half_bias, live, second_heads, head_dim, half_scale, first_heads
    )
    update = finish(attended_first, attended_second, projected, w_out)
    update = update.reshape(senders, capacity, features)
    returned = lax.all_to_all(update, axes, split_axis=0, concat_axis=0, tiled=True)
    picked = jnp.dot(
        slot_table, returned.reshape(devices * capacity, features), preferred_element_type=jnp.float32
    )
    return (cand_x.astype(jnp.float32) + picked).astype(jnp.bfloat16)


def solution(mesh):
    placed = (
        P(("req", "cache"), None),
        P(("req", "cache"), None),
        P(("req", "cache")),
        P(("req", "cache"), None),
        P(("req", "cache"), None, None, None, None),
        P(("req", "cache"), None, None, None),
        P(),
        P(),
        P(),
    )
    return jax.shard_map(
        shards, mesh=mesh, in_specs=placed, out_specs=P(("req", "cache"), None), check_vma=False
    )
```

```python
import functools
import math

import jax
import jax.numpy as jnp
from jax import lax
from jax.experimental import pallas as pl
from jax.experimental.pallas import tpu as pltpu
from jax.sharding import PartitionSpec as P


def layer_norm(values):
    average = jnp.mean(values, axis=-1, keepdims=True)
    centred = values - average
    spread = jnp.mean(centred * centred, axis=-1, keepdims=True)
    return centred * lax.rsqrt(spread + 1e-05)


def prepare(inputs, w_proj):
    normed = layer_norm(inputs.astype(jnp.float32)).astype(jnp.bfloat16)
    return jax.nn.silu(jnp.dot(normed, w_proj, preferred_element_type=jnp.float32)).astype(
        jnp.bfloat16
    )


def attend_kernel(q_ref, k_ref, v_ref, bias_ref, live_ref, o_ref, *, half_scale, chunk, first):
    head = pl.program_id(0) + first
    query = q_ref[...]
    bias_row = bias_ref[pl.ds(head, 1), :]
    event_count = k_ref.shape[0]
    acc = jnp.zeros(o_ref.shape, jnp.float32)
    for c in range(event_count // chunk):
        lo = c * chunk
        key = k_ref[pl.ds(lo, chunk), :]
        value = v_ref[pl.ds(lo, chunk), :]
        value = jnp.where(live_ref[pl.ds(lo, chunk), :] > 0.0, value, jnp.zeros_like(value))
        scores = lax.dot_general(
            query, key, (((1,), (1,)), ((), ())), preferred_element_type=jnp.float32
        )
        half = scores * half_scale + bias_row[:, lo : lo + chunk]
        weight = (half + half * jnp.tanh(half)).astype(jnp.bfloat16)
        acc = acc + jnp.dot(weight, value, preferred_element_type=jnp.float32)
    o_ref[...] = acc


def attend(projected, events, half_bias, live, head_count, head_dim, half_scale, first):
    slot_count = projected.shape[0]
    event_count = events.shape[0]
    total_heads = half_bias.shape[0]
    chunk = 512 if event_count % 512 == 0 else event_count
    kernel = functools.partial(attend_kernel, half_scale=half_scale, chunk=chunk, first=first)
    return pl.pallas_call(
        kernel,
        grid=(head_count,),
        in_specs=[
            pl.BlockSpec((slot_count, head_dim), lambda h: (0, total_heads + first + h)),
            pl.BlockSpec((event_count, head_dim), lambda h: (0, h)),
            pl.BlockSpec((event_count, head_dim), lambda h: (0, head_count + h)),
            pl.BlockSpec(half_bias.shape, lambda h: (0, 0)),
            pl.BlockSpec(live.shape, lambda h: (0, 0)),
        ],
        out_specs=pl.BlockSpec((slot_count, head_dim), lambda h: (0, h)),
        out_shape=jax.ShapeDtypeStruct((slot_count, head_count * head_dim), jnp.float32),
    )(projected, events, events, half_bias, live)


def finish_kernel(a_ref, b_ref, g_ref, w_ref, o_ref):
    attended = jnp.concatenate([a_ref[...], b_ref[...]], axis=1)
    average = jnp.mean(attended, axis=-1, keepdims=True)
    centred = attended - average
    spread = jnp.mean(centred * centred, axis=-1, keepdims=True)
    normal = centred * lax.rsqrt(spread + 1e-05)
    hidden = (normal * g_ref[...].astype(jnp.float32)).astype(jnp.bfloat16)
    o_ref[...] = jnp.dot(hidden, w_ref[...], preferred_element_type=jnp.float32).astype(o_ref.dtype)


def finish(first_half, second_half, projected, w_out):
    slot_count, first_width = first_half.shape
    second_width = second_half.shape[1]
    features = first_width + second_width
    tile = 256 if slot_count % 256 == 0 else slot_count
    return pl.pallas_call(
        finish_kernel,
        grid=(slot_count // tile,),
        in_specs=[
            pl.BlockSpec((tile, first_width), lambda i: (i, 0)),
            pl.BlockSpec((tile, second_width), lambda i: (i, 0)),
            pl.BlockSpec((tile, features), lambda i: (i, 0)),
            pl.BlockSpec(w_out.shape, lambda i: (0, 0)),
        ],
        out_specs=pl.BlockSpec((tile, w_out.shape[1]), lambda i: (i, 0)),
        out_shape=jax.ShapeDtypeStruct((slot_count, w_out.shape[1]), jnp.bfloat16),
    )(first_half, second_half, projected, w_out)


def shards(
    cand_x, cand_req, hist_len, block_place, kv_store, store_bucket, w_proj, w_out, time_bias
):
    axes = ("req", "cache")
    devices = lax.axis_size(axes)
    row_count = cand_x.shape[0]
    features = cand_x.shape[1]
    head_count = time_bias.shape[0]
    head_dim = features // head_count
    bucket_count = time_bias.shape[1]
    per_owner = kv_store.shape[2]
    block_ev = kv_store.shape[3]
    capacity = max(2, 2 * row_count // devices)
    event_count = devices * per_owner * block_ev

    target = cand_req[:, 0]
    onehot = (target[:, None] == jnp.arange(devices, dtype=jnp.int32)[None, :]).astype(jnp.int32)
    earlier = jnp.cumsum(onehot, axis=0) - onehot
    slot_rank = jnp.sum(earlier * onehot, axis=1)
    flat_slot = target * capacity + slot_rank
    slot_ids = jnp.arange(devices * capacity, dtype=jnp.int32)
    slot_table = (flat_slot[:, None] == slot_ids[None, :]).astype(cand_x.dtype)
    slotted = lax.dot_general(
        slot_table, cand_x, (((0,), (0,)), ((), ())), preferred_element_type=jnp.float32
    )
    slotted = slotted.astype(cand_x.dtype).reshape(devices, capacity, features)
    rows_per = per_owner * block_ev
    bucket_lanes = rows_per // capacity
    bucket_send = store_bucket.reshape(devices, capacity, bucket_lanes).astype(cand_x.dtype)
    bucket_send = jnp.pad(bucket_send, ((0, 0), (0, 0), (0, 128 - bucket_lanes)))
    send = jnp.concatenate([slotted, bucket_send], axis=2)
    first_heads = head_count * 3 // 4
    split = first_heads * head_dim
    kv_first = jnp.concatenate(
        [kv_store[..., :split], kv_store[..., features : features + split]], axis=-1
    )
    kv_second = jnp.concatenate(
        [kv_store[..., split:features], kv_store[..., features + split :]], axis=-1
    )
    received = lax.all_to_all(send, axes, split_axis=0, concat_axis=0, tiled=True)
    received, kv_first = lax.optimization_barrier((received, kv_first))
    arrived_first = lax.all_to_all(kv_first, axes, split_axis=1, concat_axis=0, tiled=True)
    senders = received.shape[0]
    flat_rows = received[:, :, :features].reshape(senders * capacity, features)
    buckets = received[:, :, features : features + bucket_lanes].astype(jnp.int32).reshape(event_count)

    places = block_place[0]
    block_count = places.shape[0]
    block_ids = jnp.arange(block_count, dtype=jnp.int32)
    match = (places[:, None] == block_ids[None, :]).astype(jnp.int32)
    block_of_place = jnp.sum(match * block_ids[:, None], axis=0)
    position = (
        block_of_place[:, None] * block_ev + jnp.arange(block_ev, dtype=jnp.int32)[None, :]
    ).reshape(event_count, 1)
    live = (position < hist_len[0]).astype(jnp.float32)
    bucket_table = (buckets[None, :] == jnp.arange(bucket_count, dtype=jnp.int32)[:, None]).astype(
        jnp.float32
    )
    half_bias = 0.5 * jnp.dot(time_bias, bucket_table, precision=lax.Precision.HIGHEST)
    half_scale = 0.5 / math.sqrt(head_dim)

    projected = prepare(flat_rows, w_proj)
    arrived_first, kv_second, projected, half_bias, live = lax.optimization_barrier(
        (arrived_first, kv_second, projected, half_bias, live)
    )
    arrived_second = lax.all_to_all(kv_second, axes, split_axis=1, concat_axis=0, tiled=True)
    events_first = arrived_first.reshape(event_count, 2 * split)
    events_second = arrived_second.reshape(event_count, 2 * (features - split))
    slot_count = projected.shape[0]
    attended_first = attend(
        projected, events_first, half_bias, live, first_heads, head_dim, half_scale, 0
    )
    second_heads = head_count - first_heads
    attended_second = attend(
        projected, events_second, half_bias, live, second_heads, head_dim, half_scale, first_heads
    )
    update = finish(attended_first, attended_second, projected, w_out)
    update = update.reshape(senders, capacity, features)
    returned = lax.all_to_all(update, axes, split_axis=0, concat_axis=0, tiled=True)
    picked = jnp.dot(
        slot_table, returned.reshape(devices * capacity, features), preferred_element_type=jnp.float32
    )
    return (cand_x.astype(jnp.float32) + picked).astype(jnp.bfloat16)


def solution(mesh):
    placed = (
        P(("req", "cache"), None),
        P(("req", "cache"), None),
        P(("req", "cache")),
        P(("req", "cache"), None),
        P(("req", "cache"), None, None, None, None),
        P(("req", "cache"), None, None, None),
        P(),
        P(),
        P(),
    )
    return jax.shard_map(
        shards, mesh=mesh, in_specs=placed, out_specs=P(("req", "cache"), None), check_vma=False
    )
```

```python
import functools
import math

import jax
import jax.numpy as jnp
from jax import lax
from jax.experimental import pallas as pl
from jax.experimental.pallas import tpu as pltpu
from jax.sharding import PartitionSpec as P


def layer_norm(values):
    average = jnp.mean(values, axis=-1, keepdims=True)
    centred = values - average
    spread = jnp.mean(centred * centred, axis=-1, keepdims=True)
    return centred * lax.rsqrt(spread + 1e-05)


def prepare(inputs, w_proj):
    normed = layer_norm(inputs.astype(jnp.float32)).astype(jnp.bfloat16)
    return jax.nn.silu(jnp.dot(normed, w_proj, preferred_element_type=jnp.float32)).astype(
        jnp.bfloat16
    )


def attend_kernel(q_ref, k_ref, v_ref, bias_ref, live_ref, o_ref, *, half_scale, chunk, first):
    head = pl.program_id(0) + first
    query = q_ref[...]
    bias_row = bias_ref[pl.ds(head, 1), :]
    event_count = k_ref.shape[0]
    acc = jnp.zeros(o_ref.shape, jnp.float32)
    for c in range(event_count // chunk):
        lo = c * chunk
        key = k_ref[pl.ds(lo, chunk), :]
        value = v_ref[pl.ds(lo, chunk), :]
        value = jnp.where(live_ref[pl.ds(lo, chunk), :] > 0.0, value, jnp.zeros_like(value))
        scores = lax.dot_general(
            query, key, (((1,), (1,)), ((), ())), preferred_element_type=jnp.float32
        )
        half = scores * half_scale + bias_row[:, lo : lo + chunk]
        weight = (half + half * jnp.tanh(half)).astype(jnp.bfloat16)
        acc = acc + jnp.dot(weight, value, preferred_element_type=jnp.float32)
    o_ref[...] = acc


def attend(projected, events, half_bias, live, head_count, head_dim, half_scale, first):
    slot_count = projected.shape[0]
    event_count = events.shape[0]
    total_heads = half_bias.shape[0]
    chunk = 512 if event_count % 512 == 0 else event_count
    kernel = functools.partial(attend_kernel, half_scale=half_scale, chunk=chunk, first=first)
    return pl.pallas_call(
        kernel,
        grid=(head_count,),
        in_specs=[
            pl.BlockSpec((slot_count, head_dim), lambda h: (0, total_heads + first + h)),
            pl.BlockSpec((event_count, head_dim), lambda h: (0, h)),
            pl.BlockSpec((event_count, head_dim), lambda h: (0, head_count + h)),
            pl.BlockSpec(half_bias.shape, lambda h: (0, 0)),
            pl.BlockSpec(live.shape, lambda h: (0, 0)),
        ],
        out_specs=pl.BlockSpec((slot_count, head_dim), lambda h: (0, h)),
        out_shape=jax.ShapeDtypeStruct((slot_count, head_count * head_dim), jnp.float32),
    )(projected, events, events, half_bias, live)


def finish_kernel(a_ref, b_ref, g_ref, w_ref, o_ref):
    attended = jnp.concatenate([a_ref[...], b_ref[...]], axis=1)
    average = jnp.mean(attended, axis=-1, keepdims=True)
    centred = attended - average
    spread = jnp.mean(centred * centred, axis=-1, keepdims=True)
    normal = centred * lax.rsqrt(spread + 1e-05)
    hidden = (normal * g_ref[...].astype(jnp.float32)).astype(jnp.bfloat16)
    o_ref[...] = jnp.dot(hidden, w_ref[...], preferred_element_type=jnp.float32).astype(o_ref.dtype)


def finish(first_half, second_half, projected, w_out):
    slot_count, first_width = first_half.shape
    second_width = second_half.shape[1]
    features = first_width + second_width
    tile = 256 if slot_count % 256 == 0 else slot_count
    return pl.pallas_call(
        finish_kernel,
        grid=(slot_count // tile,),
        in_specs=[
            pl.BlockSpec((tile, first_width), lambda i: (i, 0)),
            pl.BlockSpec((tile, second_width), lambda i: (i, 0)),
            pl.BlockSpec((tile, features), lambda i: (i, 0)),
            pl.BlockSpec(w_out.shape, lambda i: (0, 0)),
        ],
        out_specs=pl.BlockSpec((tile, w_out.shape[1]), lambda i: (i, 0)),
        out_shape=jax.ShapeDtypeStruct((slot_count, w_out.shape[1]), jnp.bfloat16),
    )(first_half, second_half, projected, w_out)


def shards(
    cand_x, cand_req, hist_len, block_place, kv_store, store_bucket, w_proj, w_out, time_bias
):
    axes = ("req", "cache")
    devices = lax.axis_size(axes)
    row_count = cand_x.shape[0]
    features = cand_x.shape[1]
    head_count = time_bias.shape[0]
    head_dim = features // head_count
    bucket_count = time_bias.shape[1]
    per_owner = kv_store.shape[2]
    block_ev = kv_store.shape[3]
    capacity = max(2, 2 * row_count // devices)
    event_count = devices * per_owner * block_ev

    target = cand_req[:, 0]
    onehot = (target[:, None] == jnp.arange(devices, dtype=jnp.int32)[None, :]).astype(jnp.int32)
    earlier = jnp.cumsum(onehot, axis=0) - onehot
    slot_rank = jnp.sum(earlier * onehot, axis=1)
    flat_slot = target * capacity + slot_rank
    slot_ids = jnp.arange(devices * capacity, dtype=jnp.int32)
    slot_table = (flat_slot[:, None] == slot_ids[None, :]).astype(cand_x.dtype)
    slotted = lax.dot_general(
        slot_table, cand_x, (((0,), (0,)), ((), ())), preferred_element_type=jnp.float32
    )
    slotted = slotted.astype(cand_x.dtype).reshape(devices, capacity, features)
    rows_per = per_owner * block_ev
    bucket_lanes = rows_per // capacity
    bucket_send = store_bucket.reshape(devices, capacity, bucket_lanes).astype(cand_x.dtype)
    bucket_send = jnp.pad(bucket_send, ((0, 0), (0, 0), (0, 128 - bucket_lanes)))
    send = jnp.concatenate([slotted, bucket_send], axis=2)
    first_heads = head_count - 1
    split = first_heads * head_dim
    kv_first = jnp.concatenate(
        [kv_store[..., :split], kv_store[..., features : features + split]], axis=-1
    )
    kv_second = jnp.concatenate(
        [kv_store[..., split:features], kv_store[..., features + split :]], axis=-1
    )
    received = lax.all_to_all(send, axes, split_axis=0, concat_axis=0, tiled=True)
    received, kv_first = lax.optimization_barrier((received, kv_first))
    arrived_first = lax.all_to_all(kv_first, axes, split_axis=1, concat_axis=0, tiled=True)
    senders = received.shape[0]
    flat_rows = received[:, :, :features].reshape(senders * capacity, features)
    buckets = received[:, :, features : features + bucket_lanes].astype(jnp.int32).reshape(event_count)

    places = block_place[0]
    block_count = places.shape[0]
    block_ids = jnp.arange(block_count, dtype=jnp.int32)
    match = (places[:, None] == block_ids[None, :]).astype(jnp.int32)
    block_of_place = jnp.sum(match * block_ids[:, None], axis=0)
    position = (
        block_of_place[:, None] * block_ev + jnp.arange(block_ev, dtype=jnp.int32)[None, :]
    ).reshape(event_count, 1)
    live = (position < hist_len[0]).astype(jnp.float32)
    bucket_table = (buckets[None, :] == jnp.arange(bucket_count, dtype=jnp.int32)[:, None]).astype(
        jnp.float32
    )
    half_bias = 0.5 * jnp.dot(time_bias, bucket_table, precision=lax.Precision.HIGHEST)
    half_scale = 0.5 / math.sqrt(head_dim)

    projected = prepare(flat_rows, w_proj)
    arrived_first, kv_second, projected, half_bias, live = lax.optimization_barrier(
        (arrived_first, kv_second, projected, half_bias, live)
    )
    arrived_second = lax.all_to_all(kv_second, axes, split_axis=1, concat_axis=0, tiled=True)
    events_first = arrived_first.reshape(event_count, 2 * split)
    events_second = arrived_second.reshape(event_count, 2 * (features - split))
    slot_count = projected.shape[0]
    attended_first = attend(
        projected, events_first, half_bias, live, first_heads, head_dim, half_scale, 0
    )
    second_heads = head_count - first_heads
    attended_second = attend(
        projected, events_second, half_bias, live, second_heads, head_dim, half_scale, first_heads
    )
    update = finish(attended_first, attended_second, projected, w_out)
    update = update.reshape(senders, capacity, features)
    returned = lax.all_to_all(update, axes, split_axis=0, concat_axis=0, tiled=True)
    picked = jnp.dot(
        slot_table, returned.reshape(devices * capacity, features), preferred_element_type=jnp.float32
    )
    return (cand_x.astype(jnp.float32) + picked).astype(jnp.bfloat16)


def solution(mesh):
    placed = (
        P(("req", "cache"), None),
        P(("req", "cache"), None),
        P(("req", "cache")),
        P(("req", "cache"), None),
        P(("req", "cache"), None, None, None, None),
        P(("req", "cache"), None, None, None),
        P(),
        P(),
        P(),
    )
    return jax.shard_map(
        shards, mesh=mesh, in_specs=placed, out_specs=P(("req", "cache"), None), check_vma=False
    )
```

```python
import functools
import math

import jax
import jax.numpy as jnp
from jax import lax
from jax.experimental import pallas as pl
from jax.experimental.pallas import tpu as pltpu
from jax.sharding import PartitionSpec as P


def layer_norm(values):
    average = jnp.mean(values, axis=-1, keepdims=True)
    centred = values - average
    spread = jnp.mean(centred * centred, axis=-1, keepdims=True)
    return centred * lax.rsqrt(spread + 1e-05)


def prepare(inputs, w_proj):
    normed = layer_norm(inputs.astype(jnp.float32)).astype(jnp.bfloat16)
    return jax.nn.silu(jnp.dot(normed, w_proj, preferred_element_type=jnp.float32)).astype(
        jnp.bfloat16
    )


def attend_kernel(q_ref, k_ref, v_ref, bias_ref, live_ref, o_ref, *, half_scale, chunk, first):
    head = pl.program_id(0) + first
    query = q_ref[...]
    bias_row = bias_ref[pl.ds(head, 1), :]
    event_count = k_ref.shape[0]
    acc = jnp.zeros(o_ref.shape, jnp.float32)
    for c in range(event_count // chunk):
        lo = c * chunk
        key = k_ref[pl.ds(lo, chunk), :]
        value = v_ref[pl.ds(lo, chunk), :]
        value = jnp.where(live_ref[pl.ds(lo, chunk), :] > 0.0, value, jnp.zeros_like(value))
        scores = lax.dot_general(
            query, key, (((1,), (1,)), ((), ())), preferred_element_type=jnp.float32
        )
        half = scores * half_scale + bias_row[:, lo : lo + chunk]
        weight = (half + half * jnp.tanh(half)).astype(jnp.bfloat16)
        acc = acc + jnp.dot(weight, value, preferred_element_type=jnp.float32)
    o_ref[...] = acc


def attend(projected, events, half_bias, live, head_count, head_dim, half_scale, first):
    slot_count = projected.shape[0]
    event_count = events.shape[0]
    total_heads = half_bias.shape[0]
    chunk = 512 if event_count % 512 == 0 else event_count
    kernel = functools.partial(attend_kernel, half_scale=half_scale, chunk=chunk, first=first)
    return pl.pallas_call(
        kernel,
        grid=(head_count,),
        in_specs=[
            pl.BlockSpec((slot_count, head_dim), lambda h: (0, total_heads + first + h)),
            pl.BlockSpec((event_count, head_dim), lambda h: (0, h)),
            pl.BlockSpec((event_count, head_dim), lambda h: (0, head_count + h)),
            pl.BlockSpec(half_bias.shape, lambda h: (0, 0)),
            pl.BlockSpec(live.shape, lambda h: (0, 0)),
        ],
        out_specs=pl.BlockSpec((slot_count, head_dim), lambda h: (0, h)),
        out_shape=jax.ShapeDtypeStruct((slot_count, head_count * head_dim), jnp.float32),
    )(projected, events, events, half_bias, live)


def finish_kernel(a_ref, b_ref, g_ref, w_ref, o_ref):
    attended = jnp.concatenate([a_ref[...], b_ref[...]], axis=1)
    average = jnp.mean(attended, axis=-1, keepdims=True)
    centred = attended - average
    spread = jnp.mean(centred * centred, axis=-1, keepdims=True)
    normal = centred * lax.rsqrt(spread + 1e-05)
    hidden = (normal * g_ref[...].astype(jnp.float32)).astype(jnp.bfloat16)
    o_ref[...] = jnp.dot(hidden, w_ref[...], preferred_element_type=jnp.float32).astype(o_ref.dtype)


def finish(first_half, second_half, projected, w_out):
    slot_count, first_width = first_half.shape
    second_width = second_half.shape[1]
    features = first_width + second_width
    tile = 256 if slot_count % 256 == 0 else slot_count
    return pl.pallas_call(
        finish_kernel,
        grid=(slot_count // tile,),
        in_specs=[
            pl.BlockSpec((tile, first_width), lambda i: (i, 0)),
            pl.BlockSpec((tile, second_width), lambda i: (i, 0)),
            pl.BlockSpec((tile, features), lambda i: (i, 0)),
            pl.BlockSpec(w_out.shape, lambda i: (0, 0)),
        ],
        out_specs=pl.BlockSpec((tile, w_out.shape[1]), lambda i: (i, 0)),
        out_shape=jax.ShapeDtypeStruct((slot_count, w_out.shape[1]), jnp.bfloat16),
    )(first_half, second_half, projected, w_out)


def shards(
    cand_x, cand_req, hist_len, block_place, kv_store, store_bucket, w_proj, w_out, time_bias
):
    axes = ("req", "cache")
    devices = lax.axis_size(axes)
    row_count = cand_x.shape[0]
    features = cand_x.shape[1]
    head_count = time_bias.shape[0]
    head_dim = features // head_count
    bucket_count = time_bias.shape[1]
    per_owner = kv_store.shape[2]
    block_ev = kv_store.shape[3]
    capacity = max(2, 2 * row_count // devices)
    event_count = devices * per_owner * block_ev

    target = cand_req[:, 0]
    onehot = (target[:, None] == jnp.arange(devices, dtype=jnp.int32)[None, :]).astype(jnp.int32)
    earlier = jnp.cumsum(onehot, axis=0) - onehot
    slot_rank = jnp.sum(earlier * onehot, axis=1)
    flat_slot = target * capacity + slot_rank
    slot_ids = jnp.arange(devices * capacity, dtype=jnp.int32)
    slot_table = (flat_slot[:, None] == slot_ids[None, :]).astype(cand_x.dtype)
    slotted = lax.dot_general(
        slot_table, cand_x, (((0,), (0,)), ((), ())), preferred_element_type=jnp.float32
    )
    slotted = slotted.astype(cand_x.dtype).reshape(devices, capacity, features)
    rows_per = per_owner * block_ev
    bucket_lanes = rows_per // capacity
    bucket_send = store_bucket.reshape(devices, capacity, bucket_lanes).astype(cand_x.dtype)
    bucket_send = jnp.pad(bucket_send, ((0, 0), (0, 0), (0, 128 - bucket_lanes)))
    send = jnp.concatenate([slotted, bucket_send], axis=2)
    first_heads = head_count * 5 // 8
    split = first_heads * head_dim
    kv_first = jnp.concatenate(
        [kv_store[..., :split], kv_store[..., features : features + split]], axis=-1
    )
    kv_second = jnp.concatenate(
        [kv_store[..., split:features], kv_store[..., features + split :]], axis=-1
    )
    received = lax.all_to_all(send, axes, split_axis=0, concat_axis=0, tiled=True)
    received, kv_first = lax.optimization_barrier((received, kv_first))
    arrived_first = lax.all_to_all(kv_first, axes, split_axis=1, concat_axis=0, tiled=True)
    senders = received.shape[0]
    flat_rows = received[:, :, :features].reshape(senders * capacity, features)
    buckets = received[:, :, features : features + bucket_lanes].astype(jnp.int32).reshape(event_count)

    places = block_place[0]
    block_count = places.shape[0]
    block_ids = jnp.arange(block_count, dtype=jnp.int32)
    match = (places[:, None] == block_ids[None, :]).astype(jnp.int32)
    block_of_place = jnp.sum(match * block_ids[:, None], axis=0)
    position = (
        block_of_place[:, None] * block_ev + jnp.arange(block_ev, dtype=jnp.int32)[None, :]
    ).reshape(event_count, 1)
    live = (position < hist_len[0]).astype(jnp.float32)
    bucket_table = (buckets[None, :] == jnp.arange(bucket_count, dtype=jnp.int32)[:, None]).astype(
        jnp.float32
    )
    half_bias = 0.5 * jnp.dot(time_bias, bucket_table, precision=lax.Precision.HIGHEST)
    half_scale = 0.5 / math.sqrt(head_dim)

    projected = prepare(flat_rows, w_proj)
    arrived_first, kv_second, projected, half_bias, live = lax.optimization_barrier(
        (arrived_first, kv_second, projected, half_bias, live)
    )
    arrived_second = lax.all_to_all(kv_second, axes, split_axis=1, concat_axis=0, tiled=True)
    events_first = arrived_first.reshape(event_count, 2 * split)
    events_second = arrived_second.reshape(event_count, 2 * (features - split))
    slot_count = projected.shape[0]
    attended_first = attend(
        projected, events_first, half_bias, live, first_heads, head_dim, half_scale, 0
    )
    second_heads = head_count - first_heads
    attended_second = attend(
        projected, events_second, half_bias, live, second_heads, head_dim, half_scale, first_heads
    )
    update = finish(attended_first, attended_second, projected, w_out)
    update = update.reshape(senders, capacity, features)
    returned = lax.all_to_all(update, axes, split_axis=0, concat_axis=0, tiled=True)
    picked = jnp.dot(
        slot_table, returned.reshape(devices * capacity, features), preferred_element_type=jnp.float32
    )
    return (cand_x.astype(jnp.float32) + picked).astype(jnp.bfloat16)


def solution(mesh):
    placed = (
        P(("req", "cache"), None),
        P(("req", "cache"), None),
        P(("req", "cache")),
        P(("req", "cache"), None),
        P(("req", "cache"), None, None, None, None),
        P(("req", "cache"), None, None, None),
        P(),
        P(),
        P(),
    )
    return jax.shard_map(
        shards, mesh=mesh, in_specs=placed, out_specs=P(("req", "cache"), None), check_vma=False
    )
```

```python
import functools
import math

import jax
import jax.numpy as jnp
from jax import lax
from jax.experimental import pallas as pl
from jax.experimental.pallas import tpu as pltpu
from jax.sharding import PartitionSpec as P


def layer_norm(values):
    average = jnp.mean(values, axis=-1, keepdims=True)
    centred = values - average
    spread = jnp.mean(centred * centred, axis=-1, keepdims=True)
    return centred * lax.rsqrt(spread + 1e-05)


def prepare(inputs, w_proj):
    normed = layer_norm(inputs.astype(jnp.float32)).astype(jnp.bfloat16)
    return jax.nn.silu(jnp.dot(normed, w_proj, preferred_element_type=jnp.float32)).astype(
        jnp.bfloat16
    )


def attend_kernel(q_ref, k_ref, v_ref, bias_ref, live_ref, o_ref, *, half_scale, chunk, first):
    head = pl.program_id(0) + first
    query = q_ref[...]
    bias_row = bias_ref[pl.ds(head, 1), :]
    event_count = k_ref.shape[0]
    acc = jnp.zeros(o_ref.shape, jnp.float32)
    for c in range(event_count // chunk):
        lo = c * chunk
        key = k_ref[pl.ds(lo, chunk), :]
        value = v_ref[pl.ds(lo, chunk), :]
        value = jnp.where(live_ref[pl.ds(lo, chunk), :] > 0.0, value, jnp.zeros_like(value))
        scores = lax.dot_general(
            query, key, (((1,), (1,)), ((), ())), preferred_element_type=jnp.float32
        )
        half = scores * half_scale + bias_row[:, lo : lo + chunk]
        weight = (half + half * jnp.tanh(half)).astype(jnp.bfloat16)
        acc = acc + jnp.dot(weight, value, preferred_element_type=jnp.float32)
    o_ref[...] = acc


def attend(projected, events, half_bias, live, head_count, head_dim, half_scale, first):
    slot_count = projected.shape[0]
    event_count = events.shape[0]
    total_heads = half_bias.shape[0]
    chunk = 512 if event_count % 512 == 0 else event_count
    kernel = functools.partial(attend_kernel, half_scale=half_scale, chunk=chunk, first=first)
    return pl.pallas_call(
        kernel,
        grid=(head_count,),
        in_specs=[
            pl.BlockSpec((slot_count, head_dim), lambda h: (0, total_heads + first + h)),
            pl.BlockSpec((event_count, head_dim), lambda h: (0, h)),
            pl.BlockSpec((event_count, head_dim), lambda h: (0, head_count + h)),
            pl.BlockSpec(half_bias.shape, lambda h: (0, 0)),
            pl.BlockSpec(live.shape, lambda h: (0, 0)),
        ],
        out_specs=pl.BlockSpec((slot_count, head_dim), lambda h: (0, h)),
        out_shape=jax.ShapeDtypeStruct((slot_count, head_count * head_dim), jnp.float32),
    )(projected, events, events, half_bias, live)


def finish_kernel(a_ref, b_ref, g_ref, w_ref, o_ref):
    attended = jnp.concatenate([a_ref[...], b_ref[...]], axis=1)
    average = jnp.mean(attended, axis=-1, keepdims=True)
    centred = attended - average
    spread = jnp.mean(centred * centred, axis=-1, keepdims=True)
    normal = centred * lax.rsqrt(spread + 1e-05)
    hidden = (normal * g_ref[...].astype(jnp.float32)).astype(jnp.bfloat16)
    o_ref[...] = jnp.dot(hidden, w_ref[...], preferred_element_type=jnp.float32).astype(o_ref.dtype)


def finish(first_half, second_half, projected, w_out):
    slot_count, first_width = first_half.shape
    second_width = second_half.shape[1]
    features = first_width + second_width
    tile = 128 if slot_count % 128 == 0 else slot_count
    return pl.pallas_call(
        finish_kernel,
        grid=(slot_count // tile,),
        in_specs=[
            pl.BlockSpec((tile, first_width), lambda i: (i, 0)),
            pl.BlockSpec((tile, second_width), lambda i: (i, 0)),
            pl.BlockSpec((tile, features), lambda i: (i, 0)),
            pl.BlockSpec(w_out.shape, lambda i: (0, 0)),
        ],
        out_specs=pl.BlockSpec((tile, w_out.shape[1]), lambda i: (i, 0)),
        out_shape=jax.ShapeDtypeStruct((slot_count, w_out.shape[1]), jnp.bfloat16),
    )(first_half, second_half, projected, w_out)


def shards(
    cand_x, cand_req, hist_len, block_place, kv_store, store_bucket, w_proj, w_out, time_bias
):
    axes = ("req", "cache")
    devices = lax.axis_size(axes)
    row_count = cand_x.shape[0]
    features = cand_x.shape[1]
    head_count = time_bias.shape[0]
    head_dim = features // head_count
    bucket_count = time_bias.shape[1]
    per_owner = kv_store.shape[2]
    block_ev = kv_store.shape[3]
    capacity = max(2, 2 * row_count // devices)
    event_count = devices * per_owner * block_ev

    target = cand_req[:, 0]
    onehot = (target[:, None] == jnp.arange(devices, dtype=jnp.int32)[None, :]).astype(jnp.int32)
    earlier = jnp.cumsum(onehot, axis=0) - onehot
    slot_rank = jnp.sum(earlier * onehot, axis=1)
    flat_slot = target * capacity + slot_rank
    slot_ids = jnp.arange(devices * capacity, dtype=jnp.int32)
    slot_table = (flat_slot[:, None] == slot_ids[None, :]).astype(cand_x.dtype)
    slotted = lax.dot_general(
        slot_table, cand_x, (((0,), (0,)), ((), ())), preferred_element_type=jnp.float32
    )
    slotted = slotted.astype(cand_x.dtype).reshape(devices, capacity, features)
    rows_per = per_owner * block_ev
    bucket_lanes = rows_per // capacity
    bucket_send = store_bucket.reshape(devices, capacity, bucket_lanes).astype(cand_x.dtype)
    bucket_send = jnp.pad(bucket_send, ((0, 0), (0, 0), (0, 128 - bucket_lanes)))
    send = jnp.concatenate([slotted, bucket_send], axis=2)
    first_heads = head_count * 3 // 4
    split = first_heads * head_dim
    kv_first = jnp.concatenate(
        [kv_store[..., :split], kv_store[..., features : features + split]], axis=-1
    )
    kv_second = jnp.concatenate(
        [kv_store[..., split:features], kv_store[..., features + split :]], axis=-1
    )
    received = lax.all_to_all(send, axes, split_axis=0, concat_axis=0, tiled=True)
    received, kv_first = lax.optimization_barrier((received, kv_first))
    arrived_first = lax.all_to_all(kv_first, axes, split_axis=1, concat_axis=0, tiled=True)
    senders = received.shape[0]
    flat_rows = received[:, :, :features].reshape(senders * capacity, features)
    buckets = received[:, :, features : features + bucket_lanes].astype(jnp.int32).reshape(event_count)

    places = block_place[0]
    block_count = places.shape[0]
    block_ids = jnp.arange(block_count, dtype=jnp.int32)
    match = (places[:, None] == block_ids[None, :]).astype(jnp.int32)
    block_of_place = jnp.sum(match * block_ids[:, None], axis=0)
    position = (
        block_of_place[:, None] * block_ev + jnp.arange(block_ev, dtype=jnp.int32)[None, :]
    ).reshape(event_count, 1)
    live = (position < hist_len[0]).astype(jnp.float32)
    bucket_table = (buckets[None, :] == jnp.arange(bucket_count, dtype=jnp.int32)[:, None]).astype(
        jnp.float32
    )
    half_bias = 0.5 * jnp.dot(time_bias, bucket_table, precision=lax.Precision.HIGHEST)
    half_scale = 0.5 / math.sqrt(head_dim)

    projected = prepare(flat_rows, w_proj)
    arrived_first, kv_second, projected, half_bias, live = lax.optimization_barrier(
        (arrived_first, kv_second, projected, half_bias, live)
    )
    arrived_second = lax.all_to_all(kv_second, axes, split_axis=1, concat_axis=0, tiled=True)
    events_first = arrived_first.reshape(event_count, 2 * split)
    events_second = arrived_second.reshape(event_count, 2 * (features - split))
    slot_count = projected.shape[0]
    attended_first = attend(
        projected, events_first, half_bias, live, first_heads, head_dim, half_scale, 0
    )
    second_heads = head_count - first_heads
    attended_second = attend(
        projected, events_second, half_bias, live, second_heads, head_dim, half_scale, first_heads
    )
    update = finish(attended_first, attended_second, projected, w_out)
    update = update.reshape(senders, capacity, features)
    returned = lax.all_to_all(update, axes, split_axis=0, concat_axis=0, tiled=True)
    picked = jnp.dot(
        slot_table, returned.reshape(devices * capacity, features), preferred_element_type=jnp.float32
    )
    return (cand_x.astype(jnp.float32) + picked).astype(jnp.bfloat16)


def solution(mesh):
    placed = (
        P(("req", "cache"), None),
        P(("req", "cache"), None),
        P(("req", "cache")),
        P(("req", "cache"), None),
        P(("req", "cache"), None, None, None, None),
        P(("req", "cache"), None, None, None),
        P(),
        P(),
        P(),
    )
    return jax.shard_map(
        shards, mesh=mesh, in_specs=placed, out_specs=P(("req", "cache"), None), check_vma=False
    )
```

```python
import functools
import math

import jax
import jax.numpy as jnp
from jax import lax
from jax.experimental import pallas as pl
from jax.experimental.pallas import tpu as pltpu
from jax.sharding import PartitionSpec as P


def layer_norm(values):
    average = jnp.mean(values, axis=-1, keepdims=True)
    centred = values - average
    spread = jnp.mean(centred * centred, axis=-1, keepdims=True)
    return centred * lax.rsqrt(spread + 1e-05)


def prepare(inputs, w_proj):
    normed = layer_norm(inputs.astype(jnp.float32)).astype(jnp.bfloat16)
    return jax.nn.silu(jnp.dot(normed, w_proj, preferred_element_type=jnp.float32)).astype(
        jnp.bfloat16
    )


def attend_kernel(q_ref, k_ref, v_ref, bias_ref, live_ref, o_ref, *, half_scale, chunk, first):
    head = pl.program_id(0) + first
    query = q_ref[...]
    bias_row = bias_ref[pl.ds(head, 1), :]
    event_count = k_ref.shape[0]
    acc = jnp.zeros(o_ref.shape, jnp.float32)
    for c in range(event_count // chunk):
        lo = c * chunk
        key = k_ref[pl.ds(lo, chunk), :]
        value = v_ref[pl.ds(lo, chunk), :]
        value = jnp.where(live_ref[pl.ds(lo, chunk), :] > 0.0, value, jnp.zeros_like(value))
        scores = lax.dot_general(
            query, key, (((1,), (1,)), ((), ())), preferred_element_type=jnp.float32
        )
        half = scores * half_scale + bias_row[:, lo : lo + chunk]
        weight = (half + half * jnp.tanh(half)).astype(jnp.bfloat16)
        acc = acc + jnp.dot(weight, value, preferred_element_type=jnp.float32)
    o_ref[...] = acc


def attend(projected, events, half_bias, live, head_count, head_dim, half_scale, first):
    slot_count = projected.shape[0]
    event_count = events.shape[0]
    total_heads = half_bias.shape[0]
    chunk = 1024 if event_count % 1024 == 0 else event_count
    kernel = functools.partial(attend_kernel, half_scale=half_scale, chunk=chunk, first=first)
    return pl.pallas_call(
        kernel,
        grid=(head_count,),
        in_specs=[
            pl.BlockSpec((slot_count, head_dim), lambda h: (0, total_heads + first + h)),
            pl.BlockSpec((event_count, head_dim), lambda h: (0, h)),
            pl.BlockSpec((event_count, head_dim), lambda h: (0, head_count + h)),
            pl.BlockSpec(half_bias.shape, lambda h: (0, 0)),
            pl.BlockSpec(live.shape, lambda h: (0, 0)),
        ],
        out_specs=pl.BlockSpec((slot_count, head_dim), lambda h: (0, h)),
        out_shape=jax.ShapeDtypeStruct((slot_count, head_count * head_dim), jnp.float32),
    )(projected, events, events, half_bias, live)


def finish_kernel(a_ref, b_ref, g_ref, w_ref, o_ref):
    attended = jnp.concatenate([a_ref[...], b_ref[...]], axis=1)
    average = jnp.mean(attended, axis=-1, keepdims=True)
    centred = attended - average
    spread = jnp.mean(centred * centred, axis=-1, keepdims=True)
    normal = centred * lax.rsqrt(spread + 1e-05)
    hidden = (normal * g_ref[...].astype(jnp.float32)).astype(jnp.bfloat16)
    o_ref[...] = jnp.dot(hidden, w_ref[...], preferred_element_type=jnp.float32).astype(o_ref.dtype)


def finish(first_half, second_half, projected, w_out):
    slot_count, first_width = first_half.shape
    second_width = second_half.shape[1]
    features = first_width + second_width
    tile = 256 if slot_count % 256 == 0 else slot_count
    return pl.pallas_call(
        finish_kernel,
        grid=(slot_count // tile,),
        in_specs=[
            pl.BlockSpec((tile, first_width), lambda i: (i, 0)),
            pl.BlockSpec((tile, second_width), lambda i: (i, 0)),
            pl.BlockSpec((tile, features), lambda i: (i, 0)),
            pl.BlockSpec(w_out.shape, lambda i: (0, 0)),
        ],
        out_specs=pl.BlockSpec((tile, w_out.shape[1]), lambda i: (i, 0)),
        out_shape=jax.ShapeDtypeStruct((slot_count, w_out.shape[1]), jnp.bfloat16),
    )(first_half, second_half, projected, w_out)


def shards(
    cand_x, cand_req, hist_len, block_place, kv_store, store_bucket, w_proj, w_out, time_bias
):
    axes = ("req", "cache")
    devices = lax.axis_size(axes)
    row_count = cand_x.shape[0]
    features = cand_x.shape[1]
    head_count = time_bias.shape[0]
    head_dim = features // head_count
    bucket_count = time_bias.shape[1]
    per_owner = kv_store.shape[2]
    block_ev = kv_store.shape[3]
    capacity = max(2, 2 * row_count // devices)
    event_count = devices * per_owner * block_ev

    target = cand_req[:, 0]
    onehot = (target[:, None] == jnp.arange(devices, dtype=jnp.int32)[None, :]).astype(jnp.int32)
    earlier = jnp.cumsum(onehot, axis=0) - onehot
    slot_rank = jnp.sum(earlier * onehot, axis=1)
    flat_slot = target * capacity + slot_rank
    slot_ids = jnp.arange(devices * capacity, dtype=jnp.int32)
    slot_table = (flat_slot[:, None] == slot_ids[None, :]).astype(cand_x.dtype)
    slotted = lax.dot_general(
        slot_table, cand_x, (((0,), (0,)), ((), ())), preferred_element_type=jnp.float32
    )
    slotted = slotted.astype(cand_x.dtype).reshape(devices, capacity, features)
    rows_per = per_owner * block_ev
    bucket_lanes = rows_per // capacity
    bucket_send = store_bucket.reshape(devices, capacity, bucket_lanes).astype(cand_x.dtype)
    bucket_send = jnp.pad(bucket_send, ((0, 0), (0, 0), (0, 128 - bucket_lanes)))
    send = jnp.concatenate([slotted, bucket_send], axis=2)
    first_heads = head_count * 3 // 4
    split = first_heads * head_dim
    kv_first = jnp.concatenate(
        [kv_store[..., :split], kv_store[..., features : features + split]], axis=-1
    )
    kv_second = jnp.concatenate(
        [kv_store[..., split:features], kv_store[..., features + split :]], axis=-1
    )
    received = lax.all_to_all(send, axes, split_axis=0, concat_axis=0, tiled=True)
    received, kv_first = lax.optimization_barrier((received, kv_first))
    arrived_first = lax.all_to_all(kv_first, axes, split_axis=1, concat_axis=0, tiled=True)
    senders = received.shape[0]
    flat_rows = received[:, :, :features].reshape(senders * capacity, features)
    buckets = received[:, :, features : features + bucket_lanes].astype(jnp.int32).reshape(event_count)

    places = block_place[0]
    block_count = places.shape[0]
    block_ids = jnp.arange(block_count, dtype=jnp.int32)
    match = (places[:, None] == block_ids[None, :]).astype(jnp.int32)
    block_of_place = jnp.sum(match * block_ids[:, None], axis=0)
    position = (
        block_of_place[:, None] * block_ev + jnp.arange(block_ev, dtype=jnp.int32)[None, :]
    ).reshape(event_count, 1)
    live = (position < hist_len[0]).astype(jnp.float32)
    bucket_table = (buckets[None, :] == jnp.arange(bucket_count, dtype=jnp.int32)[:, None]).astype(
        jnp.float32
    )
    half_bias = 0.5 * jnp.dot(time_bias, bucket_table, precision=lax.Precision.HIGHEST)
    half_scale = 0.5 / math.sqrt(head_dim)

    projected = prepare(flat_rows, w_proj)
    arrived_first, kv_second, projected, half_bias, live = lax.optimization_barrier(
        (arrived_first, kv_second, projected, half_bias, live)
    )
    arrived_second = lax.all_to_all(kv_second, axes, split_axis=1, concat_axis=0, tiled=True)
    events_first = arrived_first.reshape(event_count, 2 * split)
    events_second = arrived_second.reshape(event_count, 2 * (features - split))
    slot_count = projected.shape[0]
    attended_first = attend(
        projected, events_first, half_bias, live, first_heads, head_dim, half_scale, 0
    )
    second_heads = head_count - first_heads
    attended_second = attend(
        projected, events_second, half_bias, live, second_heads, head_dim, half_scale, first_heads
    )
    update = finish(attended_first, attended_second, projected, w_out)
    update = update.reshape(senders, capacity, features)
    returned = lax.all_to_all(update, axes, split_axis=0, concat_axis=0, tiled=True)
    picked = jnp.dot(
        slot_table, returned.reshape(devices * capacity, features), preferred_element_type=jnp.float32
    )
    return (cand_x.astype(jnp.float32) + picked).astype(jnp.bfloat16)


def solution(mesh):
    placed = (
        P(("req", "cache"), None),
        P(("req", "cache"), None),
        P(("req", "cache")),
        P(("req", "cache"), None),
        P(("req", "cache"), None, None, None, None),
        P(("req", "cache"), None, None, None),
        P(),
        P(),
        P(),
    )
    return jax.shard_map(
        shards, mesh=mesh, in_specs=placed, out_specs=P(("req", "cache"), None), check_vma=False
    )
```

```python
import functools
import math

import jax
import jax.numpy as jnp
from jax import lax
from jax.experimental import pallas as pl
from jax.experimental.pallas import tpu as pltpu
from jax.sharding import PartitionSpec as P


def layer_norm(values):
    average = jnp.mean(values, axis=-1, keepdims=True)
    centred = values - average
    spread = jnp.mean(centred * centred, axis=-1, keepdims=True)
    return centred * lax.rsqrt(spread + 1e-05)


def prepare(inputs, w_proj):
    normed = layer_norm(inputs.astype(jnp.float32)).astype(jnp.bfloat16)
    return jax.nn.silu(jnp.dot(normed, w_proj, preferred_element_type=jnp.float32)).astype(
        jnp.bfloat16
    )


def attend_kernel(q_ref, k_ref, v_ref, bias_ref, live_ref, o_ref, *, half_scale, chunk, first):
    head = pl.program_id(0) + first
    query = q_ref[...]
    bias_row = bias_ref[pl.ds(head, 1), :]
    event_count = k_ref.shape[0]
    acc = jnp.zeros(o_ref.shape, jnp.float32)
    for c in range(event_count // chunk):
        lo = c * chunk
        key = k_ref[pl.ds(lo, chunk), :]
        value = v_ref[pl.ds(lo, chunk), :]
        value = jnp.where(live_ref[pl.ds(lo, chunk), :] > 0.0, value, jnp.zeros_like(value))
        scores = lax.dot_general(
            query, key, (((1,), (1,)), ((), ())), preferred_element_type=jnp.float32
        )
        half = scores * half_scale + bias_row[:, lo : lo + chunk]
        weight = (half + half * jnp.tanh(half)).astype(jnp.bfloat16)
        acc = acc + jnp.dot(weight, value, preferred_element_type=jnp.float32)
    o_ref[...] = acc


def attend(projected, events, half_bias, live, head_count, head_dim, half_scale, first):
    slot_count = projected.shape[0]
    event_count = events.shape[0]
    total_heads = half_bias.shape[0]
    chunk = 512 if event_count % 512 == 0 else event_count
    kernel = functools.partial(attend_kernel, half_scale=half_scale, chunk=chunk, first=first)
    return pl.pallas_call(
        kernel,
        grid=(head_count,),
        in_specs=[
            pl.BlockSpec((slot_count, head_dim), lambda h: (0, total_heads + first + h)),
            pl.BlockSpec((event_count, head_dim), lambda h: (0, h)),
            pl.BlockSpec((event_count, head_dim), lambda h: (0, head_count + h)),
            pl.BlockSpec(half_bias.shape, lambda h: (0, 0)),
            pl.BlockSpec(live.shape, lambda h: (0, 0)),
        ],
        out_specs=pl.BlockSpec((slot_count, head_dim), lambda h: (0, h)),
        out_shape=jax.ShapeDtypeStruct((slot_count, head_count * head_dim), jnp.float32),
    )(projected, events, events, half_bias, live)


def finish_kernel(a_ref, b_ref, g_ref, w_ref, o_ref):
    attended = jnp.concatenate([a_ref[...], b_ref[...]], axis=1)
    average = jnp.mean(attended, axis=-1, keepdims=True)
    centred = attended - average
    spread = jnp.mean(centred * centred, axis=-1, keepdims=True)
    normal = centred * lax.rsqrt(spread + 1e-05)
    hidden = (normal * g_ref[...].astype(jnp.float32)).astype(jnp.bfloat16)
    o_ref[...] = jnp.dot(hidden, w_ref[...], preferred_element_type=jnp.float32).astype(o_ref.dtype)


def finish(first_half, second_half, projected, w_out):
    slot_count, first_width = first_half.shape
    second_width = second_half.shape[1]
    features = first_width + second_width
    tile = 256 if slot_count % 256 == 0 else slot_count
    return pl.pallas_call(
        finish_kernel,
        grid=(slot_count // tile,),
        in_specs=[
            pl.BlockSpec((tile, first_width), lambda i: (i, 0)),
            pl.BlockSpec((tile, second_width), lambda i: (i, 0)),
            pl.BlockSpec((tile, features), lambda i: (i, 0)),
            pl.BlockSpec(w_out.shape, lambda i: (0, 0)),
        ],
        out_specs=pl.BlockSpec((tile, w_out.shape[1]), lambda i: (i, 0)),
        out_shape=jax.ShapeDtypeStruct((slot_count, w_out.shape[1]), jnp.bfloat16),
    )(first_half, second_half, projected, w_out)


def shards(
    cand_x, cand_req, hist_len, block_place, kv_store, store_bucket, w_proj, w_out, time_bias
):
    axes = ("req", "cache")
    devices = lax.axis_size(axes)
    row_count = cand_x.shape[0]
    features = cand_x.shape[1]
    head_count = time_bias.shape[0]
    head_dim = features // head_count
    bucket_count = time_bias.shape[1]
    per_owner = kv_store.shape[2]
    block_ev = kv_store.shape[3]
    capacity = max(2, 2 * row_count // devices)
    event_count = devices * per_owner * block_ev

    target = cand_req[:, 0]
    onehot = (target[:, None] == jnp.arange(devices, dtype=jnp.int32)[None, :]).astype(jnp.bfloat16)
    row_ids = jnp.arange(row_count, dtype=jnp.int32)
    before = (row_ids[None, :] < row_ids[:, None]).astype(jnp.bfloat16)
    earlier = jnp.dot(before, onehot, preferred_element_type=jnp.float32)
    slot_rank = jnp.sum(earlier * onehot.astype(jnp.float32), axis=1).astype(jnp.int32)
    flat_slot = target * capacity + slot_rank
    slot_ids = jnp.arange(devices * capacity, dtype=jnp.int32)
    slot_table = (flat_slot[:, None] == slot_ids[None, :]).astype(cand_x.dtype)
    slotted = lax.dot_general(
        slot_table, cand_x, (((0,), (0,)), ((), ())), preferred_element_type=jnp.float32
    )
    slotted = slotted.astype(cand_x.dtype).reshape(devices, capacity, features)
    rows_per = per_owner * block_ev
    bucket_lanes = rows_per // capacity
    bucket_send = store_bucket.reshape(devices, capacity, bucket_lanes).astype(cand_x.dtype)
    bucket_send = jnp.pad(bucket_send, ((0, 0), (0, 0), (0, 128 - bucket_lanes)))
    send = jnp.concatenate([slotted, bucket_send], axis=2)
    first_heads = head_count * 3 // 4
    split = first_heads * head_dim
    kv_first = jnp.concatenate(
        [kv_store[..., :split], kv_store[..., features : features + split]], axis=-1
    )
    kv_second = jnp.concatenate(
        [kv_store[..., split:features], kv_store[..., features + split :]], axis=-1
    )
    received = lax.all_to_all(send, axes, split_axis=0, concat_axis=0, tiled=True)
    received, kv_first = lax.optimization_barrier((received, kv_first))
    arrived_first = lax.all_to_all(kv_first, axes, split_axis=1, concat_axis=0, tiled=True)
    senders = received.shape[0]
    flat_rows = received[:, :, :features].reshape(senders * capacity, features)
    buckets = received[:, :, features : features + bucket_lanes].astype(jnp.int32).reshape(event_count)

    places = block_place[0]
    block_count = places.shape[0]
    block_ids = jnp.arange(block_count, dtype=jnp.int32)
    match = (places[:, None] == block_ids[None, :]).astype(jnp.int32)
    block_of_place = jnp.sum(match * block_ids[:, None], axis=0)
    position = (
        block_of_place[:, None] * block_ev + jnp.arange(block_ev, dtype=jnp.int32)[None, :]
    ).reshape(event_count, 1)
    live = (position < hist_len[0]).astype(jnp.float32)
    bucket_table = (buckets[None, :] == jnp.arange(bucket_count, dtype=jnp.int32)[:, None]).astype(
        jnp.float32
    )
    half_bias = 0.5 * jnp.dot(time_bias, bucket_table, precision=lax.Precision.HIGHEST)
    half_scale = 0.5 / math.sqrt(head_dim)

    projected = prepare(flat_rows, w_proj)
    arrived_first, kv_second, projected, half_bias, live = lax.optimization_barrier(
        (arrived_first, kv_second, projected, half_bias, live)
    )
    arrived_second = lax.all_to_all(kv_second, axes, split_axis=1, concat_axis=0, tiled=True)
    events_first = arrived_first.reshape(event_count, 2 * split)
    events_second = arrived_second.reshape(event_count, 2 * (features - split))
    slot_count = projected.shape[0]
    attended_first = attend(
        projected, events_first, half_bias, live, first_heads, head_dim, half_scale, 0
    )
    second_heads = head_count - first_heads
    attended_second = attend(
        projected, events_second, half_bias, live, second_heads, head_dim, half_scale, first_heads
    )
    update = finish(attended_first, attended_second, projected, w_out)
    update = update.reshape(senders, capacity, features)
    returned = lax.all_to_all(update, axes, split_axis=0, concat_axis=0, tiled=True)
    picked = jnp.dot(
        slot_table, returned.reshape(devices * capacity, features), preferred_element_type=jnp.float32
    )
    return (cand_x.astype(jnp.float32) + picked).astype(jnp.bfloat16)


def solution(mesh):
    placed = (
        P(("req", "cache"), None),
        P(("req", "cache"), None),
        P(("req", "cache")),
        P(("req", "cache"), None),
        P(("req", "cache"), None, None, None, None),
        P(("req", "cache"), None, None, None),
        P(),
        P(),
        P(),
    )
    return jax.shard_map(
        shards, mesh=mesh, in_specs=placed, out_specs=P(("req", "cache"), None), check_vma=False
    )
```

```python
import functools
import math

import jax
import jax.numpy as jnp
from jax import lax
from jax.experimental import pallas as pl
from jax.experimental.pallas import tpu as pltpu
from jax.sharding import PartitionSpec as P


def layer_norm(values):
    average = jnp.mean(values, axis=-1, keepdims=True)
    centred = values - average
    spread = jnp.mean(centred * centred, axis=-1, keepdims=True)
    return centred * lax.rsqrt(spread + 1e-05)


def prepare(inputs, w_proj):
    normed = layer_norm(inputs.astype(jnp.float32)).astype(jnp.bfloat16)
    return jax.nn.silu(jnp.dot(normed, w_proj, preferred_element_type=jnp.float32)).astype(
        jnp.bfloat16
    )


def attend_kernel(q_ref, k_ref, v_ref, bias_ref, live_ref, o_ref, *, half_scale, chunk, first):
    head = pl.program_id(0) + first
    query = q_ref[...]
    bias_row = bias_ref[pl.ds(head, 1), :]
    event_count = k_ref.shape[0]
    acc = jnp.zeros(o_ref.shape, jnp.float32)
    for c in range(event_count // chunk):
        lo = c * chunk
        key = k_ref[pl.ds(lo, chunk), :]
        value = v_ref[pl.ds(lo, chunk), :]
        value = jnp.where(live_ref[pl.ds(lo, chunk), :] > 0.0, value, jnp.zeros_like(value))
        scores = lax.dot_general(
            query, key, (((1,), (1,)), ((), ())), preferred_element_type=jnp.float32
        )
        half = scores * half_scale + bias_row[:, lo : lo + chunk]
        weight = (half + half * jnp.tanh(half)).astype(jnp.bfloat16)
        acc = acc + jnp.dot(weight, value, preferred_element_type=jnp.float32)
    o_ref[...] = acc


def attend(projected, events, half_bias, live, head_count, head_dim, half_scale, first):
    slot_count = projected.shape[0]
    event_count = events.shape[0]
    total_heads = half_bias.shape[0]
    chunk = 512 if event_count % 512 == 0 else event_count
    kernel = functools.partial(attend_kernel, half_scale=half_scale, chunk=chunk, first=first)
    return pl.pallas_call(
        kernel,
        grid=(head_count,),
        in_specs=[
            pl.BlockSpec((slot_count, head_dim), lambda h: (0, total_heads + first + h)),
            pl.BlockSpec((event_count, head_dim), lambda h: (0, h)),
            pl.BlockSpec((event_count, head_dim), lambda h: (0, head_count + h)),
            pl.BlockSpec(half_bias.shape, lambda h: (0, 0)),
            pl.BlockSpec(live.shape, lambda h: (0, 0)),
        ],
        out_specs=pl.BlockSpec((slot_count, head_dim), lambda h: (0, h)),
        out_shape=jax.ShapeDtypeStruct((slot_count, head_count * head_dim), jnp.float32),
    )(projected, events, events, half_bias, live)


def finish_kernel(a_ref, b_ref, g_ref, w_ref, o_ref):
    attended = jnp.concatenate([a_ref[...], b_ref[...]], axis=1)
    average = jnp.mean(attended, axis=-1, keepdims=True)
    centred = attended - average
    spread = jnp.mean(centred * centred, axis=-1, keepdims=True)
    normal = centred * lax.rsqrt(spread + 1e-05)
    hidden = (normal * g_ref[...].astype(jnp.float32)).astype(jnp.bfloat16)
    result = jnp.dot(hidden, w_ref[...], preferred_element_type=jnp.float32).astype(o_ref.dtype)
    o_ref[...] = result.reshape(o_ref.shape)


def finish(first_half, second_half, projected, w_out):
    slot_count, first_width = first_half.shape
    second_width = second_half.shape[1]
    features = first_width + second_width
    tile = 256 if slot_count % 256 == 0 else slot_count
    return pl.pallas_call(
        finish_kernel,
        grid=(slot_count // tile,),
        in_specs=[
            pl.BlockSpec((tile, first_width), lambda i: (i, 0)),
            pl.BlockSpec((tile, second_width), lambda i: (i, 0)),
            pl.BlockSpec((tile, features), lambda i: (i, 0)),
            pl.BlockSpec(w_out.shape, lambda i: (0, 0)),
        ],
        out_specs=pl.BlockSpec((tile // 4, 4, w_out.shape[1]), lambda i: (i, 0, 0)),
        out_shape=jax.ShapeDtypeStruct((slot_count // 4, 4, w_out.shape[1]), jnp.bfloat16),
    )(first_half, second_half, projected, w_out)


def shards(
    cand_x, cand_req, hist_len, block_place, kv_store, store_bucket, w_proj, w_out, time_bias
):
    axes = ("req", "cache")
    devices = lax.axis_size(axes)
    row_count = cand_x.shape[0]
    features = cand_x.shape[1]
    head_count = time_bias.shape[0]
    head_dim = features // head_count
    bucket_count = time_bias.shape[1]
    per_owner = kv_store.shape[2]
    block_ev = kv_store.shape[3]
    capacity = max(2, 2 * row_count // devices)
    event_count = devices * per_owner * block_ev

    target = cand_req[:, 0]
    onehot = (target[:, None] == jnp.arange(devices, dtype=jnp.int32)[None, :]).astype(jnp.bfloat16)
    row_ids = jnp.arange(row_count, dtype=jnp.int32)
    before = (row_ids[None, :] < row_ids[:, None]).astype(jnp.bfloat16)
    earlier = jnp.dot(before, onehot, preferred_element_type=jnp.float32)
    slot_rank = jnp.sum(earlier * onehot.astype(jnp.float32), axis=1).astype(jnp.int32)
    flat_slot = target * capacity + slot_rank
    slot_ids = jnp.arange(devices * capacity, dtype=jnp.int32)
    slot_table = (flat_slot[:, None] == slot_ids[None, :]).astype(cand_x.dtype)
    slotted = lax.dot_general(
        slot_table, cand_x, (((0,), (0,)), ((), ())), preferred_element_type=jnp.float32
    )
    slotted = slotted.astype(cand_x.dtype).reshape(devices, capacity, features)
    rows_per = per_owner * block_ev
    bucket_lanes = rows_per // capacity
    bucket_send = store_bucket.reshape(devices, capacity, bucket_lanes).astype(cand_x.dtype)
    bucket_send = jnp.pad(bucket_send, ((0, 0), (0, 0), (0, 128 - bucket_lanes)))
    send = jnp.concatenate([slotted, bucket_send], axis=2)
    first_heads = head_count * 3 // 4
    split = first_heads * head_dim
    kv_first = jnp.concatenate(
        [kv_store[..., :split], kv_store[..., features : features + split]], axis=-1
    )
    kv_second = jnp.concatenate(
        [kv_store[..., split:features], kv_store[..., features + split :]], axis=-1
    )
    received = lax.all_to_all(send, axes, split_axis=0, concat_axis=0, tiled=True)
    received, kv_first = lax.optimization_barrier((received, kv_first))
    arrived_first = lax.all_to_all(kv_first, axes, split_axis=1, concat_axis=0, tiled=True)
    senders = received.shape[0]
    flat_rows = received[:, :, :features].reshape(senders * capacity, features)
    buckets = received[:, :, features : features + bucket_lanes].astype(jnp.int32).reshape(event_count)

    places = block_place[0]
    block_count = places.shape[0]
    block_ids = jnp.arange(block_count, dtype=jnp.int32)
    match = (places[:, None] == block_ids[None, :]).astype(jnp.int32)
    block_of_place = jnp.sum(match * block_ids[:, None], axis=0)
    position = (
        block_of_place[:, None] * block_ev + jnp.arange(block_ev, dtype=jnp.int32)[None, :]
    ).reshape(event_count, 1)
    live = (position < hist_len[0]).astype(jnp.float32)
    bucket_table = (buckets[None, :] == jnp.arange(bucket_count, dtype=jnp.int32)[:, None]).astype(
        jnp.float32
    )
    half_bias = 0.5 * jnp.dot(time_bias, bucket_table, precision=lax.Precision.HIGHEST)
    half_scale = 0.5 / math.sqrt(head_dim)

    projected = prepare(flat_rows, w_proj)
    arrived_first, kv_second, projected, half_bias, live = lax.optimization_barrier(
        (arrived_first, kv_second, projected, half_bias, live)
    )
    arrived_second = lax.all_to_all(kv_second, axes, split_axis=1, concat_axis=0, tiled=True)
    events_first = arrived_first.reshape(event_count, 2 * split)
    events_second = arrived_second.reshape(event_count, 2 * (features - split))
    slot_count = projected.shape[0]
    attended_first = attend(
        projected, events_first, half_bias, live, first_heads, head_dim, half_scale, 0
    )
    second_heads = head_count - first_heads
    attended_second = attend(
        projected, events_second, half_bias, live, second_heads, head_dim, half_scale, first_heads
    )
    update = finish(attended_first, attended_second, projected, w_out)
    update = update.reshape(senders, capacity, features)
    returned = lax.all_to_all(update, axes, split_axis=0, concat_axis=0, tiled=True)
    picked = jnp.dot(
        slot_table, returned.reshape(devices * capacity, features), preferred_element_type=jnp.float32
    )
    return (cand_x.astype(jnp.float32) + picked).astype(jnp.bfloat16)


def solution(mesh):
    placed = (
        P(("req", "cache"), None),
        P(("req", "cache"), None),
        P(("req", "cache")),
        P(("req", "cache"), None),
        P(("req", "cache"), None, None, None, None),
        P(("req", "cache"), None, None, None),
        P(),
        P(),
        P(),
    )
    return jax.shard_map(
        shards, mesh=mesh, in_specs=placed, out_specs=P(("req", "cache"), None), check_vma=False
    )
```
